128 devices in a mesh: row: 8 (over x, y_hi), col: 16 (over y_lo, z, core).
Axes of the slice: x: 4, y: 4 (y_hi: 2, y_lo: 2; y = y_hi * 2 + y_lo), z: 4, core: 2. Of those that a mesh axis runs over, the one named last changes fastest.
Arguments:
- inputs: bfloat16 [8192, 4096], P('row', 'col'), may hold values from -5 to 5
- norm_gain: float32 [4096], replicated, may hold values from 0.25 to 1.75
- query_train: float32 [4096, 4096], P(('row', 'col')), as said below
- key_train: float32 [4096, 4096], P(('row', 'col')), as said below
- value_train: float32 [4096, 4096], P(('row', 'col')), may hold values from -0.09375 to 0.09375
- out_train: float32 [4096, 2048], P(None, ('row', 'col')), may hold values from -0.09375 to 0.09375
- adapter_down: bfloat16 [4096, 128], replicated, may hold values from -0.09375 to 0.09375
- adapter_up: bfloat16 [128, 3, 32, 128], P(None, None, 'col'), may hold values from -0.5 to 0.5
- lengths: int32 [8, 7], P('row'), may hold values from 1 to 512, 1024 in all within a row
Outputs:
- mixed: bfloat16 [8192, 2048], P(('row', 'col'))
The draws below stay inside these ranges and needn't reach their ends.
Inputs may be any that keep to these rules, and one draw needn't show every extreme that they name: In each token group the 7 lengths sum to 1024; the longest is 512. `query_train`: entries are of order 1 / sqrt(4096) and at most 32 / sqrt(4096) in magnitude. `key_train`: entries are of order 1 / sqrt(4096) and at most 32 / sqrt(4096) in magnitude.
All inputs are finite; a program needn't handle non-finite values.
Results may differ from the reference program's by a relative error of at most 0.018.
Values may be sent and summed in bfloat16 or wider, within the bound.
No kernel may reach another device: no remote copies, remote signals or barrier semaphores. Data moves between devices by JAX's collectives and lax.ppermute only.
A program may use at most 128 MiB of HBM per device.

```python
import math
import jax
import jax.numpy as jnp
import numpy as np
from jax import lax

DIN = 4096
HEADS = 32
HS = 128
DOUT = 2048
RANK = 128
TOK_ROW = 1024
PROMPTS = 7
MOST = 512
GROUPS = 8
TOKENS = 8192


def own_matrix(key, label):
    own_part = jnp.clip(jax.random.normal(jax.random.fold_in(key, label), (DIN, HEADS, HS), jnp.float32), -6.0, 6.0)
    return own_part / math.sqrt(DIN)


def draw_query_train(key, part):
    result = own_matrix(key, 21)
    return result.reshape(DIN, HEADS * HS).astype(jnp.float32)


def draw_key_train(key, part):
    result = own_matrix(key, 22)
    return result.reshape(DIN, HEADS * HS).astype(jnp.float32)


def draw_inputs(key, part):
    result = jnp.clip(jax.random.normal(jax.random.fold_in(key, 34), (TOKENS, DIN), jnp.float32), -5.0, 5.0)
    return result.astype(jnp.bfloat16)


def block_scale(own_key, dims, cuts, least, high):
    level = 1.0
    for dim, shards_of in cuts:
        heights = jax.random.uniform(jax.random.fold_in(jax.random.fold_in(own_key, 6), dim), (shards_of,), jnp.float32, least / len(cuts), high / len(cuts))
        level = level * jnp.repeat(jnp.exp(heights), dims[dim] // shards_of).reshape((-1,) + (1,) * (len(dims) - 1 - dim))
    return level


def profile(amount, total, limit, lean):
    loads = [(1 << 20) // math.isqrt(grade ** lean) + 1 for grade in range(2, amount + 1)]
    surplus, counts = total - limit - (amount - 1), [1] * (amount - 1)
    while surplus > 0:
        free = [i for i in range(amount - 1) if counts[i] < limit]
        mass, left = sum([loads[i] for i in free]), surplus
        for i in free:
            more = min(limit - counts[i], max(1, left * loads[i] // mass), surplus)
            counts[i] = counts[i] + more
            surplus = surplus - more
    return np.array([limit] + counts)


def uneven_parts(rng, number_of, total, reach, skew):
    if number_of == 2:
        one = jax.random.randint(rng, (), max(1, total - reach), min(reach, total - 1) + 1)
        return jnp.stack([one, total - one])
    sizes = jnp.asarray(profile(number_of, total, reach, skew), jnp.int32)
    couples = (number_of - 1) // 2
    giver, taker = sizes[1:1 + 2 * couples:2], sizes[2:2 + 2 * couples:2]
    margin = jnp.minimum(giver - 1, reach - taker)
    passed = jax.random.randint(jax.random.fold_in(rng, 1), (couples,), 0, 1 << 20) % (margin + 1)
    sizes = sizes.at[1:1 + 2 * couples:2].set(giver - passed).at[2:2 + 2 * couples:2].set(taker + passed)
    return sizes[jax.random.permutation(jax.random.fold_in(rng, 2), number_of)]


def scatter_about(own_key, extent, deviation, most, split=(), kind=jnp.bfloat16):
    values = jax.random.normal(own_key, extent, jnp.float32) * deviation
    if len(split) > 0:
        values = block_scale(own_key, extent, split, -0.22, 0.18) * values
    return jnp.clip(values, min=-most, max=most).astype(kind)


def setup_inputs(seed: int = 0) -> dict:
    splits = jax.random.split(jax.random.key(seed), 10)
    return {
        "inputs": draw_inputs(jax.random.fold_in(splits[9], 71), 0),
        "norm_gain": jnp.clip(1.0 + 0.15 * jax.random.normal(splits[1], (DIN,), jnp.float32), 0.25, 1.75),
        "query_train": draw_query_train(jax.random.fold_in(splits[9], 71), 0),
        "key_train": draw_key_train(jax.random.fold_in(splits[9], 71), 0),
        "value_train": scatter_about(splits[4], (DIN, HEADS * HS), DIN ** -0.5, 0.09375, ((0, 128),), jnp.float32),
        "out_train": scatter_about(splits[5], (HEADS * HS, DOUT), (HEADS * HS) ** -0.5, 0.09375, ((1, 128),), jnp.float32),
        "adapter_down": scatter_about(splits[6], (DIN, RANK), DIN ** -0.5, 0.09375),
        "adapter_up": scatter_about(splits[7], (RANK, 3, HEADS, HS), RANK ** -0.5, 0.5, ((2, 16),)),
        "lengths": jax.vmap(lambda own: uneven_parts(own, PROMPTS, TOK_ROW, MOST, 2))(jax.random.split(splits[8], GROUPS)).reshape((GROUPS, PROMPTS)).astype(jnp.int32),
    }


def normalize(inputs, norm_gain):
    floats = inputs.astype(jnp.float32)
    mean_square = lax.optimization_barrier(jnp.mean(floats * floats, axis=1, keepdims=True))
    return (floats * lax.rsqrt(mean_square + 1e-05) * norm_gain).astype(jnp.bfloat16)

def segment_of(lengths_row, tok_count):
    position = jnp.arange(tok_count, dtype=jnp.int32)
    prompt_ends = jnp.cumsum(lengths_row.astype(jnp.int32))
    return lax.optimization_barrier(jnp.sum((position[:, None] >= prompt_ends[None, :]).astype(jnp.int32), axis=1))

def attend(queries, keys_all, values_all, segment):
    tok_count = queries.shape[0]
    block_rows = min(512, tok_count)
    factor = 1.0 / math.sqrt(queries.shape[2])
    key_pos = jnp.arange(tok_count, dtype=jnp.int32)
    keys_wide = keys_all.astype(jnp.float32)
    values_wide = values_all.astype(jnp.float32)

    def one_block(first):
        query_blk = lax.dynamic_slice_in_dim(queries, first, block_rows, 0).astype(jnp.float32)
        query_pos = first + jnp.arange(block_rows, dtype=jnp.int32)
        query_seg = lax.dynamic_slice_in_dim(segment, first, block_rows, 0)
        scores = jnp.einsum('qhd,khd->hqk', query_blk, keys_wide) * factor
        allowed = (query_seg[:, None] == segment[None, :]) & (key_pos[None, :] <= query_pos[:, None])
        scores = jnp.where(allowed[None], scores, -1e+30)
        highest = lax.optimization_barrier(jnp.max(scores, axis=2, keepdims=True))
        exponent = jnp.exp(scores - highest)
        weights = (exponent / lax.optimization_barrier(jnp.sum(exponent, axis=2, keepdims=True))).astype(jnp.bfloat16)
        return jnp.einsum('hqk,khd->qhd', weights.astype(jnp.float32), values_wide).astype(jnp.bfloat16)
    starts = jnp.arange(tok_count // block_rows, dtype=jnp.int32) * block_rows
    blocks = lax.map(one_block, starts)
    return blocks.reshape(tok_count, queries.shape[1] * queries.shape[2])

def reference(inputs, norm_gain, query_train, key_train, value_train, out_train, adapter_down, adapter_up, lengths):
    normed = normalize(inputs, norm_gain)
    adapted = jnp.dot(normed, adapter_down, preferred_element_type=jnp.float32).astype(jnp.bfloat16)
    projected = []
    for part_idx, trained in enumerate((query_train, key_train, value_train)):
        product = jnp.dot(normed, trained.astype(jnp.bfloat16), preferred_element_type=jnp.float32)
        adapter_term = jnp.dot(adapted, adapter_up[:, part_idx].reshape(RANK, HEADS * HS), preferred_element_type=jnp.float32)
        projected.append((product + adapter_term).astype(jnp.bfloat16).reshape(TOKENS, HEADS, HS))
    results = []
    for group_idx in range(GROUPS):
        first_row = group_idx * TOK_ROW
        segment = segment_of(lengths[group_idx], TOK_ROW)
        results.append(attend(projected[0][first_row:first_row + TOK_ROW], projected[1][first_row:first_row + TOK_ROW], projected[2][first_row:first_row + TOK_ROW], segment))
    attended = jnp.concatenate(results, axis=0)
    return jnp.dot(attended, out_train.astype(jnp.bfloat16), preferred_element_type=jnp.float32).astype(jnp.bfloat16)
```

```python
import math

import jax
import jax.numpy as jnp
from jax import lax
from jax.sharding import PartitionSpec as P

HEADS = 32
HS = 128


def normalize(whole, norm_gain):
    floats = whole.astype(jnp.float32)
    mean_square = jnp.mean(floats * floats, axis=1, keepdims=True)
    return (floats * lax.rsqrt(mean_square + 1e-05) * norm_gain).astype(jnp.bfloat16)


def segment_of(lengths_row, tok_count):
    position = jnp.arange(tok_count, dtype=jnp.int32)
    prompt_ends = jnp.cumsum(lengths_row)
    return jnp.sum((position[:, None] >= prompt_ends[None, :]).astype(jnp.int32), axis=1)


def attend(queries, keys_all, values_all, segment):
    tok_count = queries.shape[0]
    block_rows = min(512, tok_count)
    factor = 1.0 / math.sqrt(queries.shape[2])
    key_pos = jnp.arange(tok_count, dtype=jnp.int32)

    def one_block(first):
        query_blk = lax.dynamic_slice_in_dim(queries, first, block_rows, 0)
        query_pos = first + jnp.arange(block_rows, dtype=jnp.int32)
        query_seg = lax.dynamic_slice_in_dim(segment, first, block_rows, 0)
        scores = (
            jnp.einsum("qhd,khd->hqk", query_blk, keys_all, preferred_element_type=jnp.float32)
            * factor
        )
        allowed = (query_seg[:, None] == segment[None, :]) & (
            key_pos[None, :] <= query_pos[:, None]
        )
        scores = jnp.where(allowed[None], scores, -1e30)
        highest = jnp.max(scores, axis=2, keepdims=True)
        exponent = jnp.exp(scores - highest)
        weights = (exponent / jnp.sum(exponent, axis=2, keepdims=True)).astype(jnp.bfloat16)
        return jnp.einsum(
            "hqk,khd->qhd", weights, values_all, preferred_element_type=jnp.float32
        ).astype(jnp.bfloat16)

    starts = jnp.arange(tok_count // block_rows, dtype=jnp.int32) * block_rows
    blocks = lax.map(one_block, starts)
    return blocks.reshape(tok_count, queries.shape[1] * queries.shape[2])


def on_device(
    inputs,
    norm_gain,
    query_train,
    key_train,
    value_train,
    out_train,
    adapter_down,
    adapter_up,
    lengths,
):
    col_count = lax.axis_size("col")
    whole = lax.all_gather(inputs, "col", axis=1, tiled=True)
    normed = normalize(whole, norm_gain)
    tok_count = normed.shape[0]
    adapted = jnp.dot(normed, adapter_down, preferred_element_type=jnp.float32).astype(jnp.bfloat16)
    local_rows = query_train.shape[0]
    row_count = lax.axis_size("row")
    head_local = HEADS // col_count
    merged_width = 3 * head_local * HS
    trained = jnp.stack(
        (query_train.astype(jnp.bfloat16), key_train.astype(jnp.bfloat16), value_train.astype(jnp.bfloat16)),
        axis=1,
    ).reshape(local_rows, 3, col_count, head_local * HS)
    trained = jnp.transpose(trained, (2, 0, 1, 3)).reshape(col_count, local_rows, merged_width)
    sent = jnp.broadcast_to(trained[None], (row_count,) + trained.shape).reshape(
        row_count * col_count, local_rows, merged_width
    )
    merged = lax.all_to_all(sent, ("row", "col"), 0, 0, tiled=True).reshape(-1, merged_width)
    product = jnp.dot(normed, merged, preferred_element_type=jnp.float32)
    up_columns = adapter_up.reshape(adapter_up.shape[0], merged_width)
    joined = (product + jnp.dot(adapted, up_columns, preferred_element_type=jnp.float32)).astype(
        jnp.bfloat16
    )
    joined = joined.reshape(tok_count, 3, head_local, HS)
    segment = segment_of(lengths[0], tok_count)
    attended = attend(joined[:, 0], joined[:, 1], joined[:, 2], segment)
    out_local = out_train.astype(jnp.bfloat16)
    out_cols = out_local.shape[1]
    out_sent = out_local.reshape(col_count, head_local * HS, out_cols)
    out_sent = jnp.broadcast_to(out_sent[None], (row_count,) + out_sent.shape).reshape(
        row_count * col_count, head_local * HS, out_cols
    )
    out_block = lax.all_to_all(out_sent, ("row", "col"), 0, 0, tiled=True)
    out_block = jnp.transpose(out_block, (1, 0, 2)).reshape(head_local * HS, -1)
    partial_out = jnp.dot(attended, out_block, preferred_element_type=jnp.float32)
    mixed = lax.psum_scatter(
        partial_out.astype(jnp.bfloat16), "col", scatter_dimension=0, tiled=True
    )
    return mixed


def solution(mesh):
    in_specs = (
        P("row", "col"),
        P(),
        P(("row", "col"), None),
        P(("row", "col"), None),
        P(("row", "col"), None),
        P(None, ("row", "col")),
        P(),
        P(None, None, "col", None),
        P("row", None),
    )
    out_specs = P(("row", "col"), None)
    return jax.shard_map(
        on_device, mesh=mesh, in_specs=in_specs, out_specs=out_specs, check_vma=False
    )
```

```python
import math

import jax
import jax.numpy as jnp
from jax import lax
from jax.sharding import Mesh, PartitionSpec as P

HEADS = 32
HS = 128


def normalize(whole, norm_gain):
    floats = whole.astype(jnp.float32)
    mean_square = jnp.mean(floats * floats, axis=1, keepdims=True)
    return (floats * lax.rsqrt(mean_square + 1e-05) * norm_gain).astype(jnp.bfloat16)


def segment_of(lengths_row, tok_count):
    position = jnp.arange(tok_count, dtype=jnp.int32)
    prompt_ends = jnp.cumsum(lengths_row)
    return jnp.sum((position[:, None] >= prompt_ends[None, :]).astype(jnp.int32), axis=1)


def attend(queries, keys_all, values_all, segment):
    tok_count = queries.shape[0]
    block_rows = min(512, tok_count)
    factor = 1.0 / math.sqrt(queries.shape[2])
    key_pos = jnp.arange(tok_count, dtype=jnp.int32)

    def one_block(first):
        query_blk = lax.dynamic_slice_in_dim(queries, first, block_rows, 0)
        query_pos = first + jnp.arange(block_rows, dtype=jnp.int32)
        query_seg = lax.dynamic_slice_in_dim(segment, first, block_rows, 0)
        scores = (
            jnp.einsum("qhd,khd->hqk", query_blk, keys_all, preferred_element_type=jnp.float32)
            * factor
        )
        allowed = (query_seg[:, None] == segment[None, :]) & (
            key_pos[None, :] <= query_pos[:, None]
        )
        scores = jnp.where(allowed[None], scores, -1e30)
        highest = jnp.max(scores, axis=2, keepdims=True)
        exponent = jnp.exp(scores - highest)
        weights = (exponent / jnp.sum(exponent, axis=2, keepdims=True)).astype(jnp.bfloat16)
        return jnp.einsum(
            "hqk,khd->qhd", weights, values_all, preferred_element_type=jnp.float32
        ).astype(jnp.bfloat16)

    starts = jnp.arange(tok_count // block_rows, dtype=jnp.int32) * block_rows
    blocks = lax.map(one_block, starts)
    return blocks.reshape(tok_count, queries.shape[1] * queries.shape[2])


def on_device(
    inputs,
    norm_gain,
    query_train,
    key_train,
    value_train,
    out_train,
    adapter_down,
    adapter_up,
    lengths,
):
    row_count = lax.axis_size("row")
    col_count = lax.axis_size("chip") * lax.axis_size("core")
    tok_count = inputs.shape[0]
    part = lax.all_gather(inputs, "chip", axis=1, tiled=False)
    whole = lax.all_gather(part, "core", axis=2, tiled=False).reshape(tok_count, -1)
    normed = normalize(whole, norm_gain)
    adapted = jnp.dot(normed, adapter_down, preferred_element_type=jnp.float32).astype(jnp.bfloat16)
    local_rows = query_train.shape[0]
    head_local = HEADS // col_count
    merged_width = 3 * head_local * HS
    trained = jnp.stack(
        (query_train.astype(jnp.bfloat16), key_train.astype(jnp.bfloat16), value_train.astype(jnp.bfloat16)),
        axis=1,
    ).reshape(local_rows, 3, col_count, head_local * HS)
    trained = jnp.transpose(trained, (2, 0, 1, 3))
    moved = lax.all_to_all(trained, ("chip", "core"), 0, 0, tiled=True)
    moved = moved.reshape(col_count * local_rows, merged_width)
    sent = jnp.broadcast_to(moved[None], (row_count,) + moved.shape)
    merged = lax.all_to_all(sent, "row", 0, 0, tiled=True).reshape(-1, merged_width)
    product = jnp.dot(normed, merged, preferred_element_type=jnp.float32)
    up_columns = adapter_up.reshape(adapter_up.shape[0], merged_width)
    joined = (product + jnp.dot(adapted, up_columns, preferred_element_type=jnp.float32)).astype(
        jnp.bfloat16
    )
    joined = joined.reshape(tok_count, 3, head_local, HS)
    segment = segment_of(lengths[0], tok_count)
    attended = attend(joined[:, 0], joined[:, 1], joined[:, 2], segment)
    out_local = out_train.astype(jnp.bfloat16)
    out_cols = out_local.shape[1]
    out_moved = lax.all_to_all(
        out_local.reshape(col_count, head_local * HS, out_cols), ("chip", "core"), 0, 0, tiled=True
    )
    out_sent = jnp.broadcast_to(out_moved[None], (row_count,) + out_moved.shape)
    out_block = lax.all_to_all(out_sent, "row", 0, 0, tiled=True)
    out_block = jnp.transpose(out_block, (2, 0, 1, 3)).reshape(head_local * HS, -1)
    partial_out = jnp.dot(attended, out_block, preferred_element_type=jnp.float32)
    mixed = lax.psum_scatter(
        partial_out.astype(jnp.bfloat16), ("chip", "core"), scatter_dimension=0, tiled=True
    )
    return mixed


def solution(mesh):
    row_count, col_count = mesh.devices.shape
    split = Mesh(mesh.devices.reshape(row_count, col_count // 2, 2), ("row", "chip", "core"))
    col = ("chip", "core")
    in_specs = (
        P("row", col),
        P(),
        P(("row",) + col, None),
        P(("row",) + col, None),
        P(("row",) + col, None),
        P(None, ("row",) + col),
        P(),
        P(None, None, col, None),
        P("row", None),
    )
    out_specs = P(("row",) + col, None)
    return jax.shard_map(
        on_device, mesh=split, in_specs=in_specs, out_specs=out_specs, check_vma=False
    )
```

```python
import math

import jax
import jax.numpy as jnp
from jax import lax
from jax.sharding import PartitionSpec as P

HEADS = 32
HS = 128


def normalize(whole, norm_gain):
    floats = whole.astype(jnp.float32)
    mean_square = jnp.mean(floats * floats, axis=1, keepdims=True)
    return (floats * lax.rsqrt(mean_square + 1e-05) * norm_gain).astype(jnp.bfloat16)


def segment_of(lengths_row, tok_count):
    position = jnp.arange(tok_count, dtype=jnp.int32)
    prompt_ends = jnp.cumsum(lengths_row)
    return jnp.sum((position[:, None] >= prompt_ends[None, :]).astype(jnp.int32), axis=1)


def attend(queries, keys_all, values_all, segment):
    tok_count = queries.shape[0]
    block_rows = min(512, tok_count)
    factor = 1.0 / math.sqrt(queries.shape[2])
    key_pos = jnp.arange(tok_count, dtype=jnp.int32)

    def one_block(first):
        query_blk = lax.dynamic_slice_in_dim(queries, first, block_rows, 0)
        query_pos = first + jnp.arange(block_rows, dtype=jnp.int32)
        query_seg = lax.dynamic_slice_in_dim(segment, first, block_rows, 0)
        scores = (
            jnp.einsum("qhd,khd->hqk", query_blk, keys_all, preferred_element_type=jnp.float32)
            * factor
        )
        allowed = (query_seg[:, None] == segment[None, :]) & (
            key_pos[None, :] <= query_pos[:, None]
        )
        scores = jnp.where(allowed[None], scores, -1e30)
        highest = jnp.max(scores, axis=2, keepdims=True)
        exponent = jnp.exp(scores - highest)
        weights = (exponent / jnp.sum(exponent, axis=2, keepdims=True)).astype(jnp.bfloat16)
        return jnp.einsum(
            "hqk,khd->qhd", weights, values_all, preferred_element_type=jnp.float32
        ).astype(jnp.bfloat16)

    starts = jnp.arange(tok_count // block_rows, dtype=jnp.int32) * block_rows
    blocks = lax.map(one_block, starts)
    return blocks.reshape(tok_count, queries.shape[1] * queries.shape[2])


def gather_rows(block, row_count):
    row = lax.axis_index("row")
    x_count = row_count // 2
    x, y_hi = row // 2, row % 2
    pieces = [block]
    for dx in range(x_count):
        for dy in range(2):
            if dx == 0 and dy == 0:
                continue
            perm = [
                (r, ((r // 2 + dx) % x_count) * 2 + ((r % 2) ^ dy)) for r in range(row_count)
            ]
            pieces.append(lax.ppermute(block, "row", perm))
    stacked = jnp.stack(pieces)
    source = jnp.arange(row_count, dtype=jnp.int32)
    slot = ((x - source // 2) % x_count) * 2 + (y_hi ^ (source % 2))
    return jnp.take(stacked, slot, axis=0)


def scatter_sum(partial, col_count):
    col = lax.axis_index("col")
    chips = col_count // 2
    core = col % 2
    chip = col // 2
    blocks = partial.reshape(chips, 2, -1, partial.shape[1])
    keep = lax.dynamic_index_in_dim(blocks, core, 1, keepdims=False)
    give = lax.dynamic_index_in_dim(blocks, 1 - core, 1, keepdims=False)
    got = lax.ppermute(give.astype(jnp.bfloat16), "col", [(c, c ^ 1) for c in range(col_count)])
    half = keep + got.astype(jnp.float32)
    z_count = chips // 2
    total = lax.dynamic_index_in_dim(half, chip, 0, keepdims=False)
    for dz in range(z_count):
        for dy in range(2):
            if dz == 0 and dy == 0:
                continue
            def dest(c):
                cc = c // 2
                return (((cc // z_count) ^ dy) * z_count + (cc % z_count + dz) % z_count) * 2 + c % 2
            perm = [(c, dest(c)) for c in range(col_count)]
            target = ((chip // z_count) ^ dy) * z_count + (chip % z_count + dz) % z_count
            sent = lax.dynamic_index_in_dim(half, target, 0, keepdims=False).astype(jnp.bfloat16)
            total = total + lax.ppermute(sent, "col", perm).astype(jnp.float32)
    return total.astype(jnp.bfloat16)


def on_device(
    inputs,
    norm_gain,
    query_train,
    key_train,
    value_train,
    out_train,
    adapter_down,
    adapter_up,
    lengths,
):
    col_count = lax.axis_size("col")
    row_count = lax.axis_size("row")
    whole = lax.all_gather(inputs, "col", axis=1, tiled=True)
    normed = normalize(whole, norm_gain)
    tok_count = normed.shape[0]
    adapted = jnp.dot(normed, adapter_down, preferred_element_type=jnp.float32).astype(jnp.bfloat16)
    local_rows = query_train.shape[0]
    head_local = HEADS // col_count
    merged_width = 3 * head_local * HS
    trained = jnp.stack(
        (query_train.astype(jnp.bfloat16), key_train.astype(jnp.bfloat16), value_train.astype(jnp.bfloat16)),
        axis=1,
    ).reshape(local_rows, 3, col_count, head_local * HS)
    trained = jnp.transpose(trained, (2, 0, 1, 3))
    moved = lax.all_to_all(trained, "col", 0, 0, tiled=True)
    moved = moved.reshape(col_count * local_rows, merged_width)
    merged = gather_rows(moved, row_count).reshape(-1, merged_width)
    product = jnp.dot(normed, merged, preferred_element_type=jnp.float32)
    up_columns = adapter_up.reshape(adapter_up.shape[0], merged_width)
    joined = (product + jnp.dot(adapted, up_columns, preferred_element_type=jnp.float32)).astype(
        jnp.bfloat16
    )
    joined = joined.reshape(tok_count, 3, head_local, HS)
    segment = segment_of(lengths[0], tok_count)
    attended = attend(joined[:, 0], joined[:, 1], joined[:, 2], segment)
    out_local = out_train.astype(jnp.bfloat16)
    out_cols = out_local.shape[1]
    out_sent = out_local.reshape(col_count, head_local * HS, out_cols)
    out_sent = jnp.broadcast_to(out_sent[None], (row_count,) + out_sent.shape).reshape(
        row_count * col_count, head_local * HS, out_cols
    )
    out_block = lax.all_to_all(out_sent, ("row", "col"), 0, 0, tiled=True)
    out_block = jnp.transpose(out_block, (1, 0, 2)).reshape(head_local * HS, -1)
    partial_out = jnp.dot(attended, out_block, preferred_element_type=jnp.float32)
    return scatter_sum(partial_out, col_count)


def solution(mesh):
    in_specs = (
        P("row", "col"),
        P(),
        P(("row", "col"), None),
        P(("row", "col"), None),
        P(("row", "col"), None),
        P(None, ("row", "col")),
        P(),
        P(None, None, "col", None),
        P("row", None),
    )
    out_specs = P(("row", "col"), None)
    return jax.shard_map(
        on_device, mesh=mesh, in_specs=in_specs, out_specs=out_specs, check_vma=False
    )
```

```python
import math

import jax
import jax.numpy as jnp
from jax import lax
from jax.sharding import PartitionSpec as P

HEADS = 32
HS = 128


def normalize(whole, norm_gain):
    floats = whole.astype(jnp.float32)
    mean_square = jnp.mean(floats * floats, axis=1, keepdims=True)
    return (floats * lax.rsqrt(mean_square + 1e-05) * norm_gain).astype(jnp.bfloat16)


def segment_of(lengths_row, tok_count):
    position = jnp.arange(tok_count, dtype=jnp.int32)
    prompt_ends = jnp.cumsum(lengths_row)
    return jnp.sum((position[:, None] >= prompt_ends[None, :]).astype(jnp.int32), axis=1)


def attend(queries, keys_all, values_all, segment):
    tok_count = queries.shape[0]
    block_rows = min(512, tok_count)
    factor = 1.0 / math.sqrt(queries.shape[2])
    key_pos = jnp.arange(tok_count, dtype=jnp.int32)

    def one_block(first):
        query_blk = lax.dynamic_slice_in_dim(queries, first, block_rows, 0)
        query_pos = first + jnp.arange(block_rows, dtype=jnp.int32)
        query_seg = lax.dynamic_slice_in_dim(segment, first, block_rows, 0)
        scores = (
            jnp.einsum("qhd,khd->hqk", query_blk, keys_all, preferred_element_type=jnp.float32)
            * factor
        )
        allowed = (query_seg[:, None] == segment[None, :]) & (
            key_pos[None, :] <= query_pos[:, None]
        )
        scores = jnp.where(allowed[None], scores, -1e30)
        highest = jnp.max(scores, axis=2, keepdims=True)
        exponent = jnp.exp(scores - highest)
        weights = (exponent / jnp.sum(exponent, axis=2, keepdims=True)).astype(jnp.bfloat16)
        return jnp.einsum(
            "hqk,khd->qhd", weights, values_all, preferred_element_type=jnp.float32
        ).astype(jnp.bfloat16)

    starts = jnp.arange(tok_count // block_rows, dtype=jnp.int32) * block_rows
    blocks = lax.map(one_block, starts)
    return blocks.reshape(tok_count, queries.shape[1] * queries.shape[2])


def gather_rows(block, row_count):
    row = lax.axis_index("row")
    x_count = row_count // 2
    x, y_hi = row // 2, row % 2
    pieces = [block]
    for dx in range(x_count):
        for dy in range(2):
            if dx == 0 and dy == 0:
                continue
            perm = [
                (r, ((r // 2 + dx) % x_count) * 2 + ((r % 2) ^ dy)) for r in range(row_count)
            ]
            pieces.append(lax.ppermute(block, "row", perm))
    stacked = jnp.stack(pieces)
    source = jnp.arange(row_count, dtype=jnp.int32)
    slot = ((x - source // 2) % x_count) * 2 + (y_hi ^ (source % 2))
    return jnp.take(stacked, slot, axis=0)


def scatter_sum(partial, col_count):
    col = lax.axis_index("col")
    chips = col_count // 2
    core = col % 2
    chip = col // 2
    blocks = partial.reshape(chips, 2, -1, partial.shape[1])
    keep = lax.dynamic_index_in_dim(blocks, core, 1, keepdims=False)
    give = lax.dynamic_index_in_dim(blocks, 1 - core, 1, keepdims=False)
    got = lax.ppermute(give.astype(jnp.bfloat16), "col", [(c, c ^ 1) for c in range(col_count)])
    half = keep + got.astype(jnp.float32)
    z_count = chips // 2
    total = lax.dynamic_index_in_dim(half, chip, 0, keepdims=False)
    for dz in range(z_count):
        for dy in range(2):
            if dz == 0 and dy == 0:
                continue
            def dest(c):
                cc = c // 2
                return (((cc // z_count) ^ dy) * z_count + (cc % z_count + dz) % z_count) * 2 + c % 2
            perm = [(c, dest(c)) for c in range(col_count)]
            target = ((chip // z_count) ^ dy) * z_count + (chip % z_count + dz) % z_count
            sent = lax.dynamic_index_in_dim(half, target, 0, keepdims=False).astype(jnp.bfloat16)
            total = total + lax.ppermute(sent, "col", perm).astype(jnp.float32)
    return total.astype(jnp.bfloat16)


def chip_offsets(chips, dy, dz):
    z_count = chips // 2

    def move(cc):
        return ((cc // z_count) ^ dy) * z_count + (cc % z_count + dz) % z_count

    return move


def gather_cols(block, col_count):
    col = lax.axis_index("col")
    chips = col_count // 2
    z_count = chips // 2
    chip, core = col // 2, col % 2
    pieces = [block]
    sources = [chip]
    for dz in range(z_count):
        for dy in range(2):
            if dz == 0 and dy == 0:
                continue
            move = chip_offsets(chips, dy, dz)
            perm = [(c, move(c // 2) * 2 + c % 2) for c in range(col_count)]
            pieces.append(lax.ppermute(block, "col", perm))
            back = chip_offsets(chips, dy, (z_count - dz) % z_count)
            sources.append(back(chip))
    swap = [(c, c ^ 1) for c in range(col_count)]
    mates = [lax.ppermute(piece, "col", swap) for piece in pieces]
    stacked = jnp.stack(pieces + mates)
    holder = jnp.stack(sources + sources) * 2 + jnp.concatenate(
        [jnp.full((chips,), core), jnp.full((chips,), 1 - core)]
    )
    slot = jnp.argsort(holder)
    whole = jnp.take(stacked, slot, axis=0)
    return jnp.transpose(whole, (1, 0, 2)).reshape(block.shape[0], -1)


def on_device(
    inputs,
    norm_gain,
    query_train,
    key_train,
    value_train,
    out_train,
    adapter_down,
    adapter_up,
    lengths,
):
    col_count = lax.axis_size("col")
    row_count = lax.axis_size("row")
    whole = gather_cols(inputs, col_count)
    normed = normalize(whole, norm_gain)
    tok_count = normed.shape[0]
    adapted = jnp.dot(normed, adapter_down, preferred_element_type=jnp.float32).astype(jnp.bfloat16)
    local_rows = query_train.shape[0]
    head_local = HEADS // col_count
    merged_width = 3 * head_local * HS
    trained = jnp.stack(
        (query_train.astype(jnp.bfloat16), key_train.astype(jnp.bfloat16), value_train.astype(jnp.bfloat16)),
        axis=1,
    ).reshape(local_rows, 3, col_count, head_local * HS)
    trained = jnp.transpose(trained, (2, 0, 1, 3))
    moved = lax.all_to_all(trained, "col", 0, 0, tiled=True)
    moved = moved.reshape(col_count * local_rows, merged_width)
    merged = gather_rows(moved, row_count).reshape(-1, merged_width)
    product = jnp.dot(normed, merged, preferred_element_type=jnp.float32)
    up_columns = adapter_up.reshape(adapter_up.shape[0], merged_width)
    joined = (product + jnp.dot(adapted, up_columns, preferred_element_type=jnp.float32)).astype(
        jnp.bfloat16
    )
    joined = joined.reshape(tok_count, 3, head_local, HS)
    segment = segment_of(lengths[0], tok_count)
    attended = attend(joined[:, 0], joined[:, 1], joined[:, 2], segment)
    out_local = out_train.astype(jnp.bfloat16)
    out_cols = out_local.shape[1]
    out_sent = out_local.reshape(col_count, head_local * HS, out_cols)
    out_sent = jnp.broadcast_to(out_sent[None], (row_count,) + out_sent.shape).reshape(
        row_count * col_count, head_local * HS, out_cols
    )
    out_block = lax.all_to_all(out_sent, ("row", "col"), 0, 0, tiled=True)
    out_block = jnp.transpose(out_block, (1, 0, 2)).reshape(head_local * HS, -1)
    partial_out = jnp.dot(attended, out_block, preferred_element_type=jnp.float32)
    return scatter_sum(partial_out, col_count)


def solution(mesh):
    in_specs = (
        P("row", "col"),
        P(),
        P(("row", "col"), None),
        P(("row", "col"), None),
        P(("row", "col"), None),
        P(None, ("row", "col")),
        P(),
        P(None, None, "col", None),
        P("row", None),
    )
    out_specs = P(("row", "col"), None)
    return jax.shard_map(
        on_device, mesh=mesh, in_specs=in_specs, out_specs=out_specs, check_vma=False
    )
```

```python
import math

import jax
import jax.numpy as jnp
from jax import lax
from jax.sharding import PartitionSpec as P

HEADS = 32
HS = 128


def normalize(whole, norm_gain):
    floats = whole.astype(jnp.float32)
    mean_square = jnp.mean(floats * floats, axis=1, keepdims=True)
    return (floats * lax.rsqrt(mean_square + 1e-05) * norm_gain).astype(jnp.bfloat16)


def segment_of(lengths_row, tok_count):
    position = jnp.arange(tok_count, dtype=jnp.int32)
    prompt_ends = jnp.cumsum(lengths_row)
    return jnp.sum((position[:, None] >= prompt_ends[None, :]).astype(jnp.int32), axis=1)


def attend(queries, keys_all, values_all, segment):
    tok_count = queries.shape[0]
    block_rows = min(512, tok_count)
    factor = 1.0 / math.sqrt(queries.shape[2])
    key_pos = jnp.arange(tok_count, dtype=jnp.int32)

    def one_block(first):
        query_blk = lax.dynamic_slice_in_dim(queries, first, block_rows, 0)
        query_pos = first + jnp.arange(block_rows, dtype=jnp.int32)
        query_seg = lax.dynamic_slice_in_dim(segment, first, block_rows, 0)
        scores = (
            jnp.einsum("qhd,khd->hqk", query_blk, keys_all, preferred_element_type=jnp.float32)
            * factor
        )
        allowed = (query_seg[:, None] == segment[None, :]) & (
            key_pos[None, :] <= query_pos[:, None]
        )
        scores = jnp.where(allowed[None], scores, -1e30)
        highest = jnp.max(scores, axis=2, keepdims=True)
        exponent = jnp.exp(scores - highest)
        weights = (exponent / jnp.sum(exponent, axis=2, keepdims=True)).astype(jnp.bfloat16)
        return jnp.einsum(
            "hqk,khd->qhd", weights, values_all, preferred_element_type=jnp.float32
        ).astype(jnp.bfloat16)

    starts = jnp.arange(tok_count // block_rows, dtype=jnp.int32) * block_rows
    blocks = lax.map(one_block, starts)
    return blocks.reshape(tok_count, queries.shape[1] * queries.shape[2])


def gather_rows(block, row_count):
    row = lax.axis_index("row")
    x_count = row_count // 2
    x, y_hi = row // 2, row % 2
    pieces = [block]
    for dx in range(x_count):
        for dy in range(2):
            if dx == 0 and dy == 0:
                continue
            perm = [
                (r, ((r // 2 + dx) % x_count) * 2 + ((r % 2) ^ dy)) for r in range(row_count)
            ]
            pieces.append(lax.ppermute(block, "row", perm))
    stacked = jnp.stack(pieces)
    source = jnp.arange(row_count, dtype=jnp.int32)
    slot = ((x - source // 2) % x_count) * 2 + (y_hi ^ (source % 2))
    return stacked, slot


def scatter_sum(partial, col_count):
    col = lax.axis_index("col")
    chips = col_count // 2
    core = col % 2
    chip = col // 2
    blocks = partial.reshape(chips, 2, -1, partial.shape[1])
    keep = lax.dynamic_index_in_dim(blocks, core, 1, keepdims=False)
    give = lax.dynamic_index_in_dim(blocks, 1 - core, 1, keepdims=False)
    got = lax.ppermute(give.astype(jnp.bfloat16), "col", [(c, c ^ 1) for c in range(col_count)])
    half = keep + got.astype(jnp.float32)
    z_count = chips // 2
    total = lax.dynamic_index_in_dim(half, chip, 0, keepdims=False)
    for dz in range(z_count):
        for dy in range(2):
            if dz == 0 and dy == 0:
                continue
            def dest(c):
                cc = c // 2
                return (((cc // z_count) ^ dy) * z_count + (cc % z_count + dz) % z_count) * 2 + c % 2
            perm = [(c, dest(c)) for c in range(col_count)]
            target = ((chip // z_count) ^ dy) * z_count + (chip % z_count + dz) % z_count
            sent = lax.dynamic_index_in_dim(half, target, 0, keepdims=False).astype(jnp.bfloat16)
            total = total + lax.ppermute(sent, "col", perm).astype(jnp.float32)
    return total.astype(jnp.bfloat16)


def chip_offsets(chips, dy, dz):
    z_count = chips // 2

    def move(cc):
        return ((cc // z_count) ^ dy) * z_count + (cc % z_count + dz) % z_count

    return move


def gather_cols(block, col_count):
    col = lax.axis_index("col")
    chips = col_count // 2
    z_count = chips // 2
    chip, core = col // 2, col % 2
    pieces = [block]
    sources = [chip]
    for dz in range(z_count):
        for dy in range(2):
            if dz == 0 and dy == 0:
                continue
            move = chip_offsets(chips, dy, dz)
            perm = [(c, move(c // 2) * 2 + c % 2) for c in range(col_count)]
            pieces.append(lax.ppermute(block, "col", perm))
            back = chip_offsets(chips, dy, (z_count - dz) % z_count)
            sources.append(back(chip))
    swap = [(c, c ^ 1) for c in range(col_count)]
    mates = [lax.ppermute(piece, "col", swap) for piece in pieces]
    holder = jnp.stack(sources + sources) * 2 + jnp.concatenate(
        [jnp.full((chips,), core), jnp.full((chips,), 1 - core)]
    )
    return jnp.concatenate(pieces + mates, axis=1), holder


def on_device(
    inputs,
    norm_gain,
    query_train,
    key_train,
    value_train,
    out_train,
    adapter_down,
    adapter_up,
    lengths,
):
    col_count = lax.axis_size("col")
    row_count = lax.axis_size("row")
    local_rows = query_train.shape[0]
    head_local = HEADS // col_count
    merged_width = 3 * head_local * HS
    trained = jnp.stack(
        (query_train.astype(jnp.bfloat16), key_train.astype(jnp.bfloat16), value_train.astype(jnp.bfloat16)),
        axis=1,
    ).reshape(local_rows, 3, col_count, head_local * HS)
    trained = jnp.transpose(trained, (2, 0, 1, 3))
    moved = lax.all_to_all(trained, "col", 0, 0, tiled=True)
    moved = moved.reshape(col_count * local_rows, merged_width)
    stacked, slot = gather_rows(moved, row_count)
    whole, holder = gather_cols(inputs, col_count)
    block_count = holder.shape[0]
    tok_count = whole.shape[0]
    gain = jnp.take(norm_gain.reshape(block_count, -1), holder, axis=0).reshape(-1)
    down = jnp.take(
        adapter_down.reshape(block_count, -1, adapter_down.shape[1]), holder, axis=0
    ).reshape(-1, adapter_down.shape[1])
    normed = normalize(whole, gain)
    adapted = jnp.dot(normed, down, preferred_element_type=jnp.float32).astype(jnp.bfloat16)
    per_row = block_count // row_count
    blocks = stacked.reshape(row_count * per_row, -1, merged_width)
    picked = jnp.take(slot, holder // per_row) * per_row + holder % per_row
    merged = jnp.take(blocks, picked, axis=0).reshape(-1, merged_width)
    product = jnp.dot(normed, merged, preferred_element_type=jnp.float32)
    up_columns = adapter_up.reshape(adapter_up.shape[0], merged_width)
    joined = (product + jnp.dot(adapted, up_columns, preferred_element_type=jnp.float32)).astype(
        jnp.bfloat16
    )
    joined = joined.reshape(tok_count, 3, head_local, HS)
    segment = segment_of(lengths[0], tok_count)
    attended = attend(joined[:, 0], joined[:, 1], joined[:, 2], segment)
    out_local = out_train.astype(jnp.bfloat16)
    out_cols = out_local.shape[1]
    out_sent = out_local.reshape(col_count, head_local * HS, out_cols)
    out_sent = jnp.broadcast_to(out_sent[None], (row_count,) + out_sent.shape).reshape(
        row_count * col_count, head_local * HS, out_cols
    )
    out_block = lax.all_to_all(out_sent, ("row", "col"), 0, 0, tiled=True)
    out_block = jnp.transpose(out_block, (1, 0, 2)).reshape(head_local * HS, -1)
    partial_out = jnp.dot(attended, out_block, preferred_element_type=jnp.float32)
    return scatter_sum(partial_out, col_count)


def solution(mesh):
    in_specs = (
        P("row", "col"),
        P(),
        P(("row", "col"), None),
        P(("row", "col"), None),
        P(("row", "col"), None),
        P(None, ("row", "col")),
        P(),
        P(None, None, "col", None),
        P("row", None),
    )
    out_specs = P(("row", "col"), None)
    return jax.shard_map(
        on_device, mesh=mesh, in_specs=in_specs, out_specs=out_specs, check_vma=False
    )
```

```python
import math

import jax
import jax.numpy as jnp
from jax import lax
from jax.sharding import PartitionSpec as P

HEADS = 32
HS = 128


def normalize(whole, norm_gain):
    floats = whole.astype(jnp.float32)
    mean_square = jnp.mean(floats * floats, axis=1, keepdims=True)
    return (floats * lax.rsqrt(mean_square + 1e-05) * norm_gain).astype(jnp.bfloat16)


def segment_of(lengths_row, tok_count):
    position = jnp.arange(tok_count, dtype=jnp.int32)
    prompt_ends = jnp.cumsum(lengths_row)
    return jnp.sum((position[:, None] >= prompt_ends[None, :]).astype(jnp.int32), axis=1)


def attend(queries, keys_all, values_all, segment):
    tok_count = queries.shape[0]
    block_rows = min(512, tok_count)
    factor = 1.0 / math.sqrt(queries.shape[2])
    key_pos = jnp.arange(tok_count, dtype=jnp.int32)

    def one_block(first):
        query_blk = lax.dynamic_slice_in_dim(queries, first, block_rows, 0)
        query_pos = first + jnp.arange(block_rows, dtype=jnp.int32)
        query_seg = lax.dynamic_slice_in_dim(segment, first, block_rows, 0)
        scores = (
            jnp.einsum("qhd,khd->hqk", query_blk, keys_all, preferred_element_type=jnp.float32)
            * factor
        )
        allowed = (query_seg[:, None] == segment[None, :]) & (
            key_pos[None, :] <= query_pos[:, None]
        )
        scores = jnp.where(allowed[None], scores, -1e30)
        highest = jnp.max(scores, axis=2, keepdims=True)
        exponent = jnp.exp(scores - highest)
        weights = (exponent / jnp.sum(exponent, axis=2, keepdims=True)).astype(jnp.bfloat16)
        return jnp.einsum(
            "hqk,khd->qhd", weights, values_all, preferred_element_type=jnp.float32
        ).astype(jnp.bfloat16)

    starts = jnp.arange(tok_count // block_rows, dtype=jnp.int32) * block_rows
    blocks = lax.map(one_block, starts)
    return blocks.reshape(tok_count, queries.shape[1] * queries.shape[2])


def gather_rows(block, row_count):
    row = lax.axis_index("row")
    x_count = row_count // 2
    x, y_hi = row // 2, row % 2
    pieces = [block]
    for dx in range(x_count):
        for dy in range(2):
            if dx == 0 and dy == 0:
                continue
            perm = [
                (r, ((r // 2 + dx) % x_count) * 2 + ((r % 2) ^ dy)) for r in range(row_count)
            ]
            pieces.append(lax.ppermute(block, "row", perm))
    stacked = jnp.stack(pieces)
    source = jnp.arange(row_count, dtype=jnp.int32)
    slot = ((x - source // 2) % x_count) * 2 + (y_hi ^ (source % 2))
    return stacked, slot


def scatter_sum(partial, col_count):
    col = lax.axis_index("col")
    chips = col_count // 2
    core = col % 2
    chip = col // 2
    blocks = partial.reshape(chips, 2, -1, partial.shape[1])
    keep = lax.dynamic_index_in_dim(blocks, core, 1, keepdims=False)
    give = lax.dynamic_index_in_dim(blocks, 1 - core, 1, keepdims=False)
    got = lax.ppermute(give.astype(jnp.bfloat16), "col", [(c, c ^ 1) for c in range(col_count)])
    half = keep + got.astype(jnp.float32)
    z_count = chips // 2
    total = lax.dynamic_index_in_dim(half, chip, 0, keepdims=False)
    for dz in range(z_count):
        for dy in range(2):
            if dz == 0 and dy == 0:
                continue
            def dest(c):
                cc = c // 2
                return (((cc // z_count) ^ dy) * z_count + (cc % z_count + dz) % z_count) * 2 + c % 2
            perm = [(c, dest(c)) for c in range(col_count)]
            target = ((chip // z_count) ^ dy) * z_count + (chip % z_count + dz) % z_count
            sent = lax.dynamic_index_in_dim(half, target, 0, keepdims=False).astype(jnp.bfloat16)
            total = total + lax.ppermute(sent, "col", perm).astype(jnp.float32)
    return total.astype(jnp.bfloat16)


def chip_offsets(chips, dy, dz):
    z_count = chips // 2

    def move(cc):
        return ((cc // z_count) ^ dy) * z_count + (cc % z_count + dz) % z_count

    return move


def gather_cols(block, col_count):
    col = lax.axis_index("col")
    chips = col_count // 2
    z_count = chips // 2
    chip, core = col // 2, col % 2
    pieces = [block]
    sources = [chip]
    for dz in range(z_count):
        for dy in range(2):
            if dz == 0 and dy == 0:
                continue
            move = chip_offsets(chips, dy, dz)
            perm = [(c, move(c // 2) * 2 + c % 2) for c in range(col_count)]
            pieces.append(lax.ppermute(block, "col", perm))
            back = chip_offsets(chips, dy, (z_count - dz) % z_count)
            sources.append(back(chip))
    swap = [(c, c ^ 1) for c in range(col_count)]
    mates = [lax.ppermute(piece, "col", swap) for piece in pieces]
    holder = jnp.stack(sources + sources) * 2 + jnp.concatenate(
        [jnp.full((chips,), core), jnp.full((chips,), 1 - core)]
    )
    return jnp.concatenate(pieces + mates, axis=1), holder


def on_device(
    inputs,
    norm_gain,
    query_train,
    key_train,
    value_train,
    out_train,
    adapter_down,
    adapter_up,
    lengths,
):
    col_count = lax.axis_size("col")
    row_count = lax.axis_size("row")
    local_rows = query_train.shape[0]
    head_local = HEADS // col_count
    merged_width = 3 * head_local * HS
    trained = jnp.stack(
        (query_train.astype(jnp.bfloat16), key_train.astype(jnp.bfloat16), value_train.astype(jnp.bfloat16)),
        axis=1,
    ).reshape(local_rows, 3, col_count, head_local * HS)
    trained = jnp.transpose(trained, (2, 0, 1, 3))
    moved = lax.all_to_all(trained, "col", 0, 0, tiled=True)
    moved = moved.reshape(col_count * local_rows, merged_width)
    moved, inputs = lax.optimization_barrier((moved, inputs))
    stacked, slot = gather_rows(moved, row_count)
    whole, holder = gather_cols(inputs, col_count)
    block_count = holder.shape[0]
    tok_count = whole.shape[0]
    gain = jnp.take(norm_gain.reshape(block_count, -1), holder, axis=0).reshape(-1)
    down = jnp.take(
        adapter_down.reshape(block_count, -1, adapter_down.shape[1]), holder, axis=0
    ).reshape(-1, adapter_down.shape[1])
    normed = normalize(whole, gain)
    adapted = jnp.dot(normed, down, preferred_element_type=jnp.float32).astype(jnp.bfloat16)
    per_row = block_count // row_count
    blocks = stacked.reshape(row_count * per_row, -1, merged_width)
    picked = jnp.take(slot, holder // per_row) * per_row + holder % per_row
    merged = jnp.take(blocks, picked, axis=0).reshape(-1, merged_width)
    product = jnp.dot(normed, merged, preferred_element_type=jnp.float32)
    up_columns = adapter_up.reshape(adapter_up.shape[0], merged_width)
    joined = (product + jnp.dot(adapted, up_columns, preferred_element_type=jnp.float32)).astype(
        jnp.bfloat16
    )
    joined = joined.reshape(tok_count, 3, head_local, HS)
    segment = segment_of(lengths[0], tok_count)
    attended = attend(joined[:, 0], joined[:, 1], joined[:, 2], segment)
    out_local = out_train.astype(jnp.bfloat16)
    out_cols = out_local.shape[1]
    out_sent = out_local.reshape(col_count, head_local * HS, out_cols)
    out_sent = jnp.broadcast_to(out_sent[None], (row_count,) + out_sent.shape).reshape(
        row_count * col_count, head_local * HS, out_cols
    )
    out_block = lax.all_to_all(out_sent, ("row", "col"), 0, 0, tiled=True)
    out_block = jnp.transpose(out_block, (1, 0, 2)).reshape(head_local * HS, -1)
    partial_out = jnp.dot(attended, out_block, preferred_element_type=jnp.float32)
    return scatter_sum(partial_out, col_count)


def solution(mesh):
    in_specs = (
        P("row", "col"),
        P(),
        P(("row", "col"), None),
        P(("row", "col"), None),
        P(("row", "col"), None),
        P(None, ("row", "col")),
        P(),
        P(None, None, "col", None),
        P("row", None),
    )
    out_specs = P(("row", "col"), None)
    return jax.shard_map(
        on_device, mesh=mesh, in_specs=in_specs, out_specs=out_specs, check_vma=False
    )
```

```python
import math

import jax
import jax.numpy as jnp
from jax import lax
from jax.sharding import PartitionSpec as P

HEADS = 32
HS = 128


def normalize(whole, norm_gain):
    floats = whole.astype(jnp.float32)
    mean_square = jnp.mean(floats * floats, axis=1, keepdims=True)
    return (floats * lax.rsqrt(mean_square + 1e-05) * norm_gain).astype(jnp.bfloat16)


def segment_of(lengths_row, tok_count):
    position = jnp.arange(tok_count, dtype=jnp.int32)
    prompt_ends = jnp.cumsum(lengths_row)
    return jnp.sum((position[:, None] >= prompt_ends[None, :]).astype(jnp.int32), axis=1)


def attend(queries, keys_all, values_all, segment):
    tok_count = queries.shape[0]
    block_rows = min(512, tok_count)
    factor = 1.0 / math.sqrt(queries.shape[2])
    key_pos = jnp.arange(tok_count, dtype=jnp.int32)

    def one_block(first):
        query_blk = lax.dynamic_slice_in_dim(queries, first, block_rows, 0)
        query_pos = first + jnp.arange(block_rows, dtype=jnp.int32)
        query_seg = lax.dynamic_slice_in_dim(segment, first, block_rows, 0)
        scores = (
            jnp.einsum("qhd,khd->hqk", query_blk, keys_all, preferred_element_type=jnp.float32)
            * factor
        )
        allowed = (query_seg[:, None] == segment[None, :]) & (
            key_pos[None, :] <= query_pos[:, None]
        )
        scores = jnp.where(allowed[None], scores, -1e30)
        highest = jnp.max(scores, axis=2, keepdims=True)
        exponent = jnp.exp(scores - highest)
        weights = (exponent / jnp.sum(exponent, axis=2, keepdims=True)).astype(jnp.bfloat16)
        return jnp.einsum(
            "hqk,khd->qhd", weights, values_all, preferred_element_type=jnp.float32
        ).astype(jnp.bfloat16)

    starts = jnp.arange(tok_count // block_rows, dtype=jnp.int32) * block_rows
    blocks = lax.map(one_block, starts)
    return blocks.reshape(tok_count, queries.shape[1] * queries.shape[2])


def gather_rows(block, row_count):
    row = lax.axis_index("row")
    x_count = row_count // 2
    x, side = row // 2, row % 2
    half = block.shape[0] // 2

    def rid(xx, ss):
        return (xx % x_count) * 2 + ss

    def send(value, dx):
        perm = [(r, rid(r // 2 + dx, r % 2)) for r in range(row_count)]
        return lax.ppermute(value, "row", perm)

    from_minus = send(block, 1)
    from_plus = send(block, -1)
    from_y = lax.ppermute(block, "row", [(r, r ^ 1) for r in range(row_count)])
    got_minus = send(jnp.concatenate([from_minus[:half], from_y]), 1)
    got_plus = send(jnp.concatenate([from_plus[half:], from_y]), -1)
    last_minus = send(got_minus[half : half + half], 1)
    last_plus = send(got_plus[half + half :], -1)
    pieces = [
        block,
        from_minus,
        from_plus,
        from_y,
        jnp.concatenate([got_minus[:half], got_plus[:half]]),
        got_minus[half:],
        got_plus[half:],
        jnp.concatenate([last_minus, last_plus]),
    ]
    sources = jnp.stack(
        [
            rid(x, side),
            rid(x - 1, side),
            rid(x + 1, side),
            rid(x, 1 - side),
            rid(x + 2, side),
            rid(x - 1, 1 - side),
            rid(x + 1, 1 - side),
            rid(x + 2, 1 - side),
        ]
    )
    return jnp.stack(pieces), jnp.argsort(sources)


def scatter_sum(partial, col_count):
    col = lax.axis_index("col")
    chips = col_count // 2
    core = col % 2
    chip = col // 2
    blocks = partial.reshape(chips, 2, -1, partial.shape[1])
    keep = lax.dynamic_index_in_dim(blocks, core, 1, keepdims=False)
    give = lax.dynamic_index_in_dim(blocks, 1 - core, 1, keepdims=False)
    got = lax.ppermute(give.astype(jnp.bfloat16), "col", [(c, c ^ 1) for c in range(col_count)])
    half = keep + got.astype(jnp.float32)
    z_count = chips // 2
    total = lax.dynamic_index_in_dim(half, chip, 0, keepdims=False)
    for dz in range(z_count):
        for dy in range(2):
            if dz == 0 and dy == 0:
                continue
            def dest(c):
                cc = c // 2
                return (((cc // z_count) ^ dy) * z_count + (cc % z_count + dz) % z_count) * 2 + c % 2
            perm = [(c, dest(c)) for c in range(col_count)]
            target = ((chip // z_count) ^ dy) * z_count + (chip % z_count + dz) % z_count
            sent = lax.dynamic_index_in_dim(half, target, 0, keepdims=False).astype(jnp.bfloat16)
            total = total + lax.ppermute(sent, "col", perm).astype(jnp.float32)
    return total.astype(jnp.bfloat16)


def chip_offsets(chips, dy, dz):
    z_count = chips // 2

    def move(cc):
        return ((cc // z_count) ^ dy) * z_count + (cc % z_count + dz) % z_count

    return move


def gather_cols(block, col_count):
    col = lax.axis_index("col")
    chips = col_count // 2
    z_count = chips // 2
    chip, core = col // 2, col % 2
    pieces = [block]
    sources = [chip]
    for dz in range(z_count):
        for dy in range(2):
            if dz == 0 and dy == 0:
                continue
            move = chip_offsets(chips, dy, dz)
            perm = [(c, move(c // 2) * 2 + c % 2) for c in range(col_count)]
            pieces.append(lax.ppermute(block, "col", perm))
            back = chip_offsets(chips, dy, (z_count - dz) % z_count)
            sources.append(back(chip))
    swap = [(c, c ^ 1) for c in range(col_count)]
    mates = [lax.ppermute(piece, "col", swap) for piece in pieces]
    holder = jnp.stack(sources + sources) * 2 + jnp.concatenate(
        [jnp.full((chips,), core), jnp.full((chips,), 1 - core)]
    )
    return jnp.concatenate(pieces + mates, axis=1), holder


def on_device(
    inputs,
    norm_gain,
    query_train,
    key_train,
    value_train,
    out_train,
    adapter_down,
    adapter_up,
    lengths,
):
    col_count = lax.axis_size("col")
    row_count = lax.axis_size("row")
    local_rows = query_train.shape[0]
    head_local = HEADS // col_count
    merged_width = 3 * head_local * HS
    trained = jnp.stack(
        (query_train.astype(jnp.bfloat16), key_train.astype(jnp.bfloat16), value_train.astype(jnp.bfloat16)),
        axis=1,
    ).reshape(local_rows, 3, col_count, head_local * HS)
    trained = jnp.transpose(trained, (2, 0, 1, 3))
    moved = lax.all_to_all(trained, "col", 0, 0, tiled=True)
    moved = moved.reshape(col_count * local_rows, merged_width)
    moved, inputs = lax.optimization_barrier((moved, inputs))
    stacked, slot = gather_rows(moved, row_count)
    whole, holder = gather_cols(inputs, col_count)
    block_count = holder.shape[0]
    tok_count = whole.shape[0]
    gain = jnp.take(norm_gain.reshape(block_count, -1), holder, axis=0).reshape(-1)
    down = jnp.take(
        adapter_down.reshape(block_count, -1, adapter_down.shape[1]), holder, axis=0
    ).reshape(-1, adapter_down.shape[1])
    normed = normalize(whole, gain)
    adapted = jnp.dot(normed, down, preferred_element_type=jnp.float32).astype(jnp.bfloat16)
    per_row = block_count // row_count
    blocks = stacked.reshape(row_count * per_row, -1, merged_width)
    picked = jnp.take(slot, holder // per_row) * per_row + holder % per_row
    merged = jnp.take(blocks, picked, axis=0).reshape(-1, merged_width)
    product = jnp.dot(normed, merged, preferred_element_type=jnp.float32)
    up_columns = adapter_up.reshape(adapter_up.shape[0], merged_width)
    joined = (product + jnp.dot(adapted, up_columns, preferred_element_type=jnp.float32)).astype(
        jnp.bfloat16
    )
    joined = joined.reshape(tok_count, 3, head_local, HS)
    segment = segment_of(lengths[0], tok_count)
    attended = attend(joined[:, 0], joined[:, 1], joined[:, 2], segment)
    out_local = out_train.astype(jnp.bfloat16)
    out_cols = out_local.shape[1]
    out_sent = out_local.reshape(col_count, head_local * HS, out_cols)
    out_sent = jnp.broadcast_to(out_sent[None], (row_count,) + out_sent.shape).reshape(
        row_count * col_count, head_local * HS, out_cols
    )
    out_block = lax.all_to_all(out_sent, ("row", "col"), 0, 0, tiled=True)
    out_block = jnp.transpose(out_block, (1, 0, 2)).reshape(head_local * HS, -1)
    partial_out = jnp.dot(attended, out_block, preferred_element_type=jnp.float32)
    return scatter_sum(partial_out, col_count)


def solution(mesh):
    in_specs = (
        P("row", "col"),
        P(),
        P(("row", "col"), None),
        P(("row", "col"), None),
        P(("row", "col"), None),
        P(None, ("row", "col")),
        P(),
        P(None, None, "col", None),
        P("row", None),
    )
    out_specs = P(("row", "col"), None)
    return jax.shard_map(
        on_device, mesh=mesh, in_specs=in_specs, out_specs=out_specs, check_vma=False
    )
```

```python
import math

import jax
import jax.numpy as jnp
from jax import lax
from jax.sharding import PartitionSpec as P

HEADS = 32
HS = 128


def normalize(whole, norm_gain):
    floats = whole.astype(jnp.float32)
    mean_square = jnp.mean(floats * floats, axis=1, keepdims=True)
    return (floats * lax.rsqrt(mean_square + 1e-05) * norm_gain).astype(jnp.bfloat16)


def segment_of(lengths_row, tok_count):
    position = jnp.arange(tok_count, dtype=jnp.int32)
    prompt_ends = jnp.cumsum(lengths_row)
    return jnp.sum((position[:, None] >= prompt_ends[None, :]).astype(jnp.int32), axis=1)


def attend(queries, keys_all, values_all, segment):
    tok_count = queries.shape[0]
    block_rows = min(512, tok_count)
    factor = 1.0 / math.sqrt(queries.shape[2])
    key_pos = jnp.arange(tok_count, dtype=jnp.int32)

    def one_block(first):
        query_blk = lax.dynamic_slice_in_dim(queries, first, block_rows, 0)
        query_pos = first + jnp.arange(block_rows, dtype=jnp.int32)
        query_seg = lax.dynamic_slice_in_dim(segment, first, block_rows, 0)
        scores = (
            jnp.einsum("qhd,khd->hqk", query_blk, keys_all, preferred_element_type=jnp.float32)
            * factor
        )
        allowed = (query_seg[:, None] == segment[None, :]) & (
            key_pos[None, :] <= query_pos[:, None]
        )
        scores = jnp.where(allowed[None], scores, -1e30)
        highest = jnp.max(scores, axis=2, keepdims=True)
        exponent = jnp.exp(scores - highest)
        weights = (exponent / jnp.sum(exponent, axis=2, keepdims=True)).astype(jnp.bfloat16)
        return jnp.einsum(
            "hqk,khd->qhd", weights, values_all, preferred_element_type=jnp.float32
        ).astype(jnp.bfloat16)

    starts = jnp.arange(tok_count // block_rows, dtype=jnp.int32) * block_rows
    blocks = lax.map(one_block, starts)
    return blocks.reshape(tok_count, queries.shape[1] * queries.shape[2])


def ring_gather(block, axis, count, place, index):
    me = lax.axis_index(axis)
    ring, side = place(me)
    half = block.shape[0] // 2

    def send(value, step):
        perm = []
        for i in range(count):
            pos, sd = place(i)
            perm.append((i, index(pos + step, sd, i)))
        return lax.ppermute(value, axis, perm)

    def flip(value):
        perm = []
        for i in range(count):
            pos, sd = place(i)
            perm.append((i, index(pos, 1 - sd, i)))
        return lax.ppermute(value, axis, perm)

    from_minus = send(block, 1)
    from_plus = send(block, -1)
    from_y = flip(block)
    got_minus = send(jnp.concatenate([from_minus[:half], from_y]), 1)
    got_plus = send(jnp.concatenate([from_plus[half:], from_y]), -1)
    last_minus = send(got_minus[half : half + half], 1)
    last_plus = send(got_plus[half + half :], -1)
    pieces = [
        block,
        from_minus,
        from_plus,
        from_y,
        jnp.concatenate([got_minus[:half], got_plus[:half]]),
        got_minus[half:],
        got_plus[half:],
        jnp.concatenate([last_minus, last_plus]),
    ]
    sources = [
        index(ring, side, me),
        index(ring - 1, side, me),
        index(ring + 1, side, me),
        index(ring, 1 - side, me),
        index(ring + 2, side, me),
        index(ring - 1, 1 - side, me),
        index(ring + 1, 1 - side, me),
        index(ring + 2, 1 - side, me),
    ]
    return pieces, sources


def gather_rows(block, row_count):
    pieces, sources = ring_gather(
        block,
        "row",
        row_count,
        lambda r: (r // 2, r % 2),
        lambda pos, sd, r: (pos % 4) * 2 + sd,
    )
    return jnp.stack(pieces), jnp.argsort(jnp.stack(sources))


def scatter_sum(partial, col_count):
    col = lax.axis_index("col")
    chips = col_count // 2
    core = col % 2
    chip = col // 2
    blocks = partial.reshape(chips, 2, -1, partial.shape[1])
    keep = lax.dynamic_index_in_dim(blocks, core, 1, keepdims=False)
    give = lax.dynamic_index_in_dim(blocks, 1 - core, 1, keepdims=False)
    got = lax.ppermute(give.astype(jnp.bfloat16), "col", [(c, c ^ 1) for c in range(col_count)])
    half = keep + got.astype(jnp.float32)
    z_count = chips // 2
    total = lax.dynamic_index_in_dim(half, chip, 0, keepdims=False)
    for dz in range(z_count):
        for dy in range(2):
            if dz == 0 and dy == 0:
                continue
            def dest(c):
                cc = c // 2
                return (((cc // z_count) ^ dy) * z_count + (cc % z_count + dz) % z_count) * 2 + c % 2
            perm = [(c, dest(c)) for c in range(col_count)]
            target = ((chip // z_count) ^ dy) * z_count + (chip % z_count + dz) % z_count
            sent = lax.dynamic_index_in_dim(half, target, 0, keepdims=False).astype(jnp.bfloat16)
            total = total + lax.ppermute(sent, "col", perm).astype(jnp.float32)
    return total.astype(jnp.bfloat16)


def chip_offsets(chips, dy, dz):
    z_count = chips // 2

    def move(cc):
        return ((cc // z_count) ^ dy) * z_count + (cc % z_count + dz) % z_count

    return move


def gather_cols(block, col_count):
    core = lax.axis_index("col") % 2
    pieces, sources = ring_gather(
        block,
        "col",
        col_count,
        lambda c: ((c // 2) % 4, (c // 2) // 4),
        lambda pos, sd, c: (sd * 4 + pos % 4) * 2 + c % 2,
    )
    swap = [(c, c ^ 1) for c in range(col_count)]
    mates = [lax.ppermute(piece, "col", swap) for piece in pieces]
    chips = jnp.stack(sources) // 2
    holder = jnp.concatenate([chips * 2 + core, chips * 2 + 1 - core])
    return jnp.concatenate(pieces + mates, axis=1), holder


def on_device(
    inputs,
    norm_gain,
    query_train,
    key_train,
    value_train,
    out_train,
    adapter_down,
    adapter_up,
    lengths,
):
    col_count = lax.axis_size("col")
    row_count = lax.axis_size("row")
    local_rows = query_train.shape[0]
    head_local = HEADS // col_count
    merged_width = 3 * head_local * HS
    trained = jnp.stack(
        (query_train.astype(jnp.bfloat16), key_train.astype(jnp.bfloat16), value_train.astype(jnp.bfloat16)),
        axis=1,
    ).reshape(local_rows, 3, col_count, head_local * HS)
    trained = jnp.transpose(trained, (2, 0, 1, 3))
    moved = lax.all_to_all(trained, "col", 0, 0, tiled=True)
    moved = moved.reshape(col_count * local_rows, merged_width)
    moved, inputs = lax.optimization_barrier((moved, inputs))
    stacked, slot = gather_rows(moved, row_count)
    whole, holder = gather_cols(inputs, col_count)
    block_count = holder.shape[0]
    tok_count = whole.shape[0]
    gain = jnp.take(norm_gain.reshape(block_count, -1), holder, axis=0).reshape(-1)
    down = jnp.take(
        adapter_down.reshape(block_count, -1, adapter_down.shape[1]), holder, axis=0
    ).reshape(-1, adapter_down.shape[1])
    normed = normalize(whole, gain)
    adapted = jnp.dot(normed, down, preferred_element_type=jnp.float32).astype(jnp.bfloat16)
    per_row = block_count // row_count
    blocks = stacked.reshape(row_count * per_row, -1, merged_width)
    picked = jnp.take(slot, holder // per_row) * per_row + holder % per_row
    merged = jnp.take(blocks, picked, axis=0).reshape(-1, merged_width)
    product = jnp.dot(normed, merged, preferred_element_type=jnp.float32)
    up_columns = adapter_up.reshape(adapter_up.shape[0], merged_width)
    joined = (product + jnp.dot(adapted, up_columns, preferred_element_type=jnp.float32)).astype(
        jnp.bfloat16
    )
    joined = joined.reshape(tok_count, 3, head_local, HS)
    segment = segment_of(lengths[0], tok_count)
    attended = attend(joined[:, 0], joined[:, 1], joined[:, 2], segment)
    out_local = out_train.astype(jnp.bfloat16)
    out_cols = out_local.shape[1]
    out_sent = out_local.reshape(col_count, head_local * HS, out_cols)
    out_sent = jnp.broadcast_to(out_sent[None], (row_count,) + out_sent.shape).reshape(
        row_count * col_count, head_local * HS, out_cols
    )
    out_block = lax.all_to_all(out_sent, ("row", "col"), 0, 0, tiled=True)
    out_block = jnp.transpose(out_block, (1, 0, 2)).reshape(head_local * HS, -1)
    partial_out = jnp.dot(attended, out_block, preferred_element_type=jnp.float32)
    return scatter_sum(partial_out, col_count)


def solution(mesh):
    in_specs = (
        P("row", "col"),
        P(),
        P(("row", "col"), None),
        P(("row", "col"), None),
        P(("row", "col"), None),
        P(None, ("row", "col")),
        P(),
        P(None, None, "col", None),
        P("row", None),
    )
    out_specs = P(("row", "col"), None)
    return jax.shard_map(
        on_device, mesh=mesh, in_specs=in_specs, out_specs=out_specs, check_vma=False
    )
```

```python
import math

import jax
import jax.numpy as jnp
from jax import lax
from jax.sharding import PartitionSpec as P

HEADS = 32
HS = 128


def normalize(whole, norm_gain):
    floats = whole.astype(jnp.float32)
    mean_square = jnp.mean(floats * floats, axis=1, keepdims=True)
    return (floats * lax.rsqrt(mean_square + 1e-05) * norm_gain).astype(jnp.bfloat16)


def segment_of(lengths_row, tok_count):
    position = jnp.arange(tok_count, dtype=jnp.int32)
    prompt_ends = jnp.cumsum(lengths_row)
    return jnp.sum((position[:, None] >= prompt_ends[None, :]).astype(jnp.int32), axis=1)


def attend(queries, keys_all, values_all, segment):
    tok_count = queries.shape[0]
    block_rows = min(512, tok_count)
    factor = 1.0 / math.sqrt(queries.shape[2])
    key_pos = jnp.arange(tok_count, dtype=jnp.int32)

    def one_block(first):
        query_blk = lax.dynamic_slice_in_dim(queries, first, block_rows, 0)
        query_pos = first + jnp.arange(block_rows, dtype=jnp.int32)
        query_seg = lax.dynamic_slice_in_dim(segment, first, block_rows, 0)
        scores = (
            jnp.einsum("qhd,khd->hqk", query_blk, keys_all, preferred_element_type=jnp.float32)
            * factor
        )
        allowed = (query_seg[:, None] == segment[None, :]) & (
            key_pos[None, :] <= query_pos[:, None]
        )
        scores = jnp.where(allowed[None], scores, -1e30)
        highest = jnp.max(scores, axis=2, keepdims=True)
        exponent = jnp.exp(scores - highest)
        weights = (exponent / jnp.sum(exponent, axis=2, keepdims=True)).astype(jnp.bfloat16)
        return jnp.einsum(
            "hqk,khd->qhd", weights, values_all, preferred_element_type=jnp.float32
        ).astype(jnp.bfloat16)

    starts = jnp.arange(tok_count // block_rows, dtype=jnp.int32) * block_rows
    blocks = lax.map(one_block, starts)
    return blocks.reshape(tok_count, queries.shape[1] * queries.shape[2])


def ring_gather(block, axis, count, place, index):
    me = lax.axis_index(axis)
    ring, side = place(me)
    half = block.shape[0] // 2

    def send(value, step):
        perm = []
        for i in range(count):
            pos, sd = place(i)
            perm.append((i, index(pos + step, sd, i)))
        return lax.ppermute(value, axis, perm)

    def flip(value):
        perm = []
        for i in range(count):
            pos, sd = place(i)
            perm.append((i, index(pos, 1 - sd, i)))
        return lax.ppermute(value, axis, perm)

    from_minus = send(block, 1)
    from_plus = send(block, -1)
    from_y = flip(block)
    got_minus = send(jnp.concatenate([from_minus[:half], from_y]), 1)
    got_plus = send(jnp.concatenate([from_plus[half:], from_y]), -1)
    last_minus = send(got_minus[half : half + half], 1)
    last_plus = send(got_plus[half + half :], -1)
    pieces = [
        block,
        from_minus,
        from_plus,
        from_y,
        jnp.concatenate([got_minus[:half], got_plus[:half]]),
        got_minus[half:],
        got_plus[half:],
        jnp.concatenate([last_minus, last_plus]),
    ]
    sources = [
        index(ring, side, me),
        index(ring - 1, side, me),
        index(ring + 1, side, me),
        index(ring, 1 - side, me),
        index(ring + 2, side, me),
        index(ring - 1, 1 - side, me),
        index(ring + 1, 1 - side, me),
        index(ring + 2, 1 - side, me),
    ]
    return pieces, sources


def gather_rows(block, row_count):
    pieces, sources = ring_gather(
        block,
        "row",
        row_count,
        lambda r: (r // 2, r % 2),
        lambda pos, sd, r: (pos % 4) * 2 + sd,
    )
    return jnp.stack(pieces), jnp.argsort(jnp.stack(sources))


def scatter_sum(partial, col_count):
    col = lax.axis_index("col")
    chips = col_count // 2
    core = col % 2
    chip = col // 2
    blocks = partial.reshape(chips, 2, -1, partial.shape[1])
    keep = lax.dynamic_index_in_dim(blocks, core, 1, keepdims=False)
    give = lax.dynamic_index_in_dim(blocks, 1 - core, 1, keepdims=False)
    got = lax.ppermute(give.astype(jnp.bfloat16), "col", [(c, c ^ 1) for c in range(col_count)])
    half = keep + got.astype(jnp.float32)
    z_count = chips // 2
    total = lax.dynamic_index_in_dim(half, chip, 0, keepdims=False)
    for dz in range(z_count):
        for dy in range(2):
            if dz == 0 and dy == 0:
                continue
            def dest(c):
                cc = c // 2
                return (((cc // z_count) ^ dy) * z_count + (cc % z_count + dz) % z_count) * 2 + c % 2
            perm = [(c, dest(c)) for c in range(col_count)]
            target = ((chip // z_count) ^ dy) * z_count + (chip % z_count + dz) % z_count
            sent = lax.dynamic_index_in_dim(half, target, 0, keepdims=False).astype(jnp.bfloat16)
            total = total + lax.ppermute(sent, "col", perm).astype(jnp.float32)
    return total.astype(jnp.bfloat16)


def chip_offsets(chips, dy, dz):
    z_count = chips // 2

    def move(cc):
        return ((cc // z_count) ^ dy) * z_count + (cc % z_count + dz) % z_count

    return move


def gather_cols(block, col_count):
    core = lax.axis_index("col") % 2
    pieces, sources = ring_gather(
        block,
        "col",
        col_count,
        lambda c: ((c // 2) % 4, (c // 2) // 4),
        lambda pos, sd, c: (sd * 4 + pos % 4) * 2 + c % 2,
    )
    swap = [(c, c ^ 1) for c in range(col_count)]
    mates = [lax.ppermute(piece, "col", swap) for piece in pieces]
    chips = jnp.stack(sources) // 2
    holder = jnp.concatenate([chips * 2 + core, chips * 2 + 1 - core])
    return jnp.concatenate(pieces + mates, axis=1), holder


def on_device(
    inputs,
    norm_gain,
    query_train,
    key_train,
    value_train,
    out_train,
    adapter_down,
    adapter_up,
    lengths,
):
    col_count = lax.axis_size("col")
    row_count = lax.axis_size("row")
    local_rows = query_train.shape[0]
    head_local = HEADS // col_count
    merged_width = 3 * head_local * HS
    trained = jnp.stack(
        (query_train.astype(jnp.bfloat16), key_train.astype(jnp.bfloat16), value_train.astype(jnp.bfloat16)),
        axis=1,
    ).reshape(local_rows, 3, col_count, head_local * HS)
    trained = jnp.transpose(trained, (2, 0, 1, 3))
    moved = lax.all_to_all(trained, "col", 0, 0, tiled=True)
    moved = moved.reshape(col_count * local_rows, merged_width)
    moved, inputs = lax.optimization_barrier((moved, inputs))
    stacked, slot = gather_rows(moved, row_count)
    whole, holder = gather_cols(inputs, col_count)
    block_count = holder.shape[0]
    tok_count = whole.shape[0]
    gain = jnp.take(norm_gain.reshape(block_count, -1), holder, axis=0).reshape(-1)
    down = jnp.take(
        adapter_down.reshape(block_count, -1, adapter_down.shape[1]), holder, axis=0
    ).reshape(-1, adapter_down.shape[1])
    normed = normalize(whole, gain)
    adapted = jnp.dot(normed, down, preferred_element_type=jnp.float32).astype(jnp.bfloat16)
    per_row = block_count // row_count
    blocks = stacked.reshape(row_count * per_row, -1, merged_width)
    picked = jnp.take(slot, holder // per_row) * per_row + holder % per_row
    merged = jnp.take(blocks, picked, axis=0).reshape(-1, merged_width)
    product = jnp.dot(normed, merged, preferred_element_type=jnp.float32)
    up_columns = adapter_up.reshape(adapter_up.shape[0], merged_width)
    joined = (product + jnp.dot(adapted, up_columns, preferred_element_type=jnp.float32)).astype(
        jnp.bfloat16
    )
    joined = joined.reshape(tok_count, 3, head_local, HS)
    segment = segment_of(lengths[0], tok_count)
    attended = attend(joined[:, 0], joined[:, 1], joined[:, 2], segment)
    out_local, normed = lax.optimization_barrier((out_train, normed))
    out_local = out_local.astype(jnp.bfloat16)
    out_cols = out_local.shape[1]
    out_sent = out_local.reshape(col_count, head_local * HS, out_cols)
    out_sent = jnp.broadcast_to(out_sent[None], (row_count,) + out_sent.shape).reshape(
        row_count * col_count, head_local * HS, out_cols
    )
    out_block = lax.all_to_all(out_sent, ("row", "col"), 0, 0, tiled=True)
    out_block = jnp.transpose(out_block, (1, 0, 2)).reshape(head_local * HS, -1)
    partial_out = jnp.dot(attended, out_block, preferred_element_type=jnp.float32)
    return scatter_sum(partial_out, col_count)


def solution(mesh):
    in_specs = (
        P("row", "col"),
        P(),
        P(("row", "col"), None),
        P(("row", "col"), None),
        P(("row", "col"), None),
        P(None, ("row", "col")),
        P(),
        P(None, None, "col", None),
        P("row", None),
    )
    out_specs = P(("row", "col"), None)
    return jax.shard_map(
        on_device, mesh=mesh, in_specs=in_specs, out_specs=out_specs, check_vma=False
    )
```

```python
import math

import jax
import jax.numpy as jnp
from jax import lax
from jax.sharding import PartitionSpec as P

HEADS = 32
HS = 128


def normalize(whole, norm_gain):
    floats = whole.astype(jnp.float32)
    mean_square = jnp.mean(floats * floats, axis=1, keepdims=True)
    return (floats * lax.rsqrt(mean_square + 1e-05) * norm_gain).astype(jnp.bfloat16)


def segment_of(lengths_row, tok_count):
    position = jnp.arange(tok_count, dtype=jnp.int32)
    prompt_ends = jnp.cumsum(lengths_row)
    return jnp.sum((position[:, None] >= prompt_ends[None, :]).astype(jnp.int32), axis=1)


def attend(queries, keys_all, values_all, segment):
    tok_count = queries.shape[0]
    block_rows = min(512, tok_count)
    factor = 1.0 / math.sqrt(queries.shape[2])
    key_pos = jnp.arange(tok_count, dtype=jnp.int32)

    def one_block(first):
        query_blk = lax.dynamic_slice_in_dim(queries, first, block_rows, 0)
        query_pos = first + jnp.arange(block_rows, dtype=jnp.int32)
        query_seg = lax.dynamic_slice_in_dim(segment, first, block_rows, 0)
        scores = (
            jnp.einsum("qhd,khd->hqk", query_blk, keys_all, preferred_element_type=jnp.float32)
            * factor
        )
        allowed = (query_seg[:, None] == segment[None, :]) & (
            key_pos[None, :] <= query_pos[:, None]
        )
        scores = jnp.where(allowed[None], scores, -1e30)
        highest = jnp.max(scores, axis=2, keepdims=True)
        exponent = jnp.exp(scores - highest)
        weights = (exponent / jnp.sum(exponent, axis=2, keepdims=True)).astype(jnp.bfloat16)
        return jnp.einsum(
            "hqk,khd->qhd", weights, values_all, preferred_element_type=jnp.float32
        ).astype(jnp.bfloat16)

    starts = jnp.arange(tok_count // block_rows, dtype=jnp.int32) * block_rows
    blocks = lax.map(one_block, starts)
    return blocks.reshape(tok_count, queries.shape[1] * queries.shape[2])


def ring_gather(block, axis, count, place, index):
    me = lax.axis_index(axis)
    ring, side = place(me)
    half = block.shape[0] // 2

    def send(value, step):
        perm = []
        for i in range(count):
            pos, sd = place(i)
            perm.append((i, index(pos + step, sd, i)))
        return lax.ppermute(value, axis, perm)

    def flip(value):
        perm = []
        for i in range(count):
            pos, sd = place(i)
            perm.append((i, index(pos, 1 - sd, i)))
        return lax.ppermute(value, axis, perm)

    from_minus = send(block, 1)
    from_plus = send(block, -1)
    from_y = flip(block)
    got_minus = send(jnp.concatenate([from_minus[:half], from_y]), 1)
    got_plus = send(jnp.concatenate([from_plus[half:], from_y]), -1)
    last_minus = send(got_minus[half : half + half], 1)
    last_plus = send(got_plus[half + half :], -1)
    pieces = [
        block,
        from_minus,
        from_plus,
        from_y,
        jnp.concatenate([got_minus[:half], got_plus[:half]]),
        got_minus[half:],
        got_plus[half:],
        jnp.concatenate([last_minus, last_plus]),
    ]
    sources = [
        index(ring, side, me),
        index(ring - 1, side, me),
        index(ring + 1, side, me),
        index(ring, 1 - side, me),
        index(ring + 2, side, me),
        index(ring - 1, 1 - side, me),
        index(ring + 1, 1 - side, me),
        index(ring + 2, 1 - side, me),
    ]
    return pieces, sources


def gather_rows(block, row_count):
    pieces, sources = ring_gather(
        block,
        "row",
        row_count,
        lambda r: (r // 2, r % 2),
        lambda pos, sd, r: (pos % 4) * 2 + sd,
    )
    return jnp.stack(pieces), jnp.argsort(jnp.stack(sources))


def scatter_sum(partial, col_count):
    col = lax.axis_index("col")
    chips = col_count // 2
    core = col % 2
    chip = col // 2
    blocks = partial.reshape(chips, 2, -1, partial.shape[1])
    keep = lax.dynamic_index_in_dim(blocks, core, 1, keepdims=False)
    give = lax.dynamic_index_in_dim(blocks, 1 - core, 1, keepdims=False)
    got = lax.ppermute(give.astype(jnp.bfloat16), "col", [(c, c ^ 1) for c in range(col_count)])
    half = keep + got.astype(jnp.float32)
    z_count = chips // 2
    total = lax.dynamic_index_in_dim(half, chip, 0, keepdims=False)
    for dz in range(z_count):
        for dy in range(2):
            if dz == 0 and dy == 0:
                continue
            def dest(c):
                cc = c // 2
                return (((cc // z_count) ^ dy) * z_count + (cc % z_count + dz) % z_count) * 2 + c % 2
            perm = [(c, dest(c)) for c in range(col_count)]
            target = ((chip // z_count) ^ dy) * z_count + (chip % z_count + dz) % z_count
            sent = lax.dynamic_index_in_dim(half, target, 0, keepdims=False).astype(jnp.bfloat16)
            total = total + lax.ppermute(sent, "col", perm).astype(jnp.float32)
    return total.astype(jnp.bfloat16)


def chip_offsets(chips, dy, dz):
    z_count = chips // 2

    def move(cc):
        return ((cc // z_count) ^ dy) * z_count + (cc % z_count + dz) % z_count

    return move


def gather_cols(block, col_count):
    core = lax.axis_index("col") % 2
    pieces, sources = ring_gather(
        block,
        "col",
        col_count,
        lambda c: ((c // 2) % 4, (c // 2) // 4),
        lambda pos, sd, c: (sd * 4 + pos % 4) * 2 + c % 2,
    )
    swap = [(c, c ^ 1) for c in range(col_count)]
    mates = [lax.ppermute(piece, "col", swap) for piece in pieces]
    chips = jnp.stack(sources) // 2
    holder = jnp.concatenate([chips * 2 + core, chips * 2 + 1 - core])
    return jnp.concatenate(pieces + mates, axis=1), holder


def on_device(
    inputs,
    norm_gain,
    query_train,
    key_train,
    value_train,
    out_train,
    adapter_down,
    adapter_up,
    lengths,
):
    col_count = lax.axis_size("col")
    row_count = lax.axis_size("row")
    local_rows = query_train.shape[0]
    head_local = HEADS // col_count
    merged_width = 3 * head_local * HS
    trained = jnp.stack(
        (query_train.astype(jnp.bfloat16), key_train.astype(jnp.bfloat16), value_train.astype(jnp.bfloat16)),
        axis=1,
    ).reshape(local_rows, 3, col_count, head_local * HS)
    trained = jnp.transpose(trained, (2, 0, 1, 3)).reshape(col_count, -1)
    out_local = out_train.astype(jnp.bfloat16)
    out_cols = out_local.shape[1]
    both = jnp.concatenate([trained, out_local.reshape(col_count, -1)], axis=1)
    both = lax.all_to_all(both, "col", 0, 0, tiled=True)
    moved = both[:, : trained.shape[1]].reshape(col_count * local_rows, merged_width)
    out_moved = both[:, trained.shape[1] :].reshape(col_count, head_local * HS, out_cols)
    out_moved = jnp.transpose(out_moved, (1, 0, 2)).reshape(head_local * HS, -1)
    moved, inputs = lax.optimization_barrier((moved, inputs))
    stacked, slot = gather_rows(moved, row_count)
    whole, holder = gather_cols(inputs, col_count)
    block_count = holder.shape[0]
    tok_count = whole.shape[0]
    gain = jnp.take(norm_gain.reshape(block_count, -1), holder, axis=0).reshape(-1)
    down = jnp.take(
        adapter_down.reshape(block_count, -1, adapter_down.shape[1]), holder, axis=0
    ).reshape(-1, adapter_down.shape[1])
    normed = normalize(whole, gain)
    adapted = jnp.dot(normed, down, preferred_element_type=jnp.float32).astype(jnp.bfloat16)
    per_row = block_count // row_count
    blocks = stacked.reshape(row_count * per_row, -1, merged_width)
    picked = jnp.take(slot, holder // per_row) * per_row + holder % per_row
    merged = jnp.take(blocks, picked, axis=0).reshape(-1, merged_width)
    product = jnp.dot(normed, merged, preferred_element_type=jnp.float32)
    up_columns = adapter_up.reshape(adapter_up.shape[0], merged_width)
    joined = (product + jnp.dot(adapted, up_columns, preferred_element_type=jnp.float32)).astype(
        jnp.bfloat16
    )
    joined = joined.reshape(tok_count, 3, head_local, HS)
    segment = segment_of(lengths[0], tok_count)
    attended = attend(joined[:, 0], joined[:, 1], joined[:, 2], segment)
    out_stack, out_slot = gather_rows(out_moved, row_count)
    out_block = jnp.take(out_stack, out_slot, axis=0)
    out_block = jnp.transpose(out_block, (1, 0, 2)).reshape(head_local * HS, -1)
    partial_out = jnp.dot(attended, out_block, preferred_element_type=jnp.float32)
    return scatter_sum(partial_out, col_count)


def solution(mesh):
    in_specs = (
        P("row", "col"),
        P(),
        P(("row", "col"), None),
        P(("row", "col"), None),
        P(("row", "col"), None),
        P(None, ("row", "col")),
        P(),
        P(None, None, "col", None),
        P("row", None),
    )
    out_specs = P(("row", "col"), None)
    return jax.shard_map(
        on_device, mesh=mesh, in_specs=in_specs, out_specs=out_specs, check_vma=False
    )
```

```python
import math

import jax
import jax.numpy as jnp
from jax import lax
from jax.sharding import PartitionSpec as P

HEADS = 32
HS = 128


def normalize(whole, norm_gain):
    floats = whole.astype(jnp.float32)
    mean_square = jnp.mean(floats * floats, axis=1, keepdims=True)
    return (floats * lax.rsqrt(mean_square + 1e-05) * norm_gain).astype(jnp.bfloat16)


def segment_of(lengths_row, tok_count):
    position = jnp.arange(tok_count, dtype=jnp.int32)
    prompt_ends = jnp.cumsum(lengths_row)
    return jnp.sum((position[:, None] >= prompt_ends[None, :]).astype(jnp.int32), axis=1)


def attend(queries, keys_all, values_all, segment):
    tok_count = queries.shape[0]
    block_rows = min(512, tok_count)
    factor = 1.0 / math.sqrt(queries.shape[2])
    key_pos = jnp.arange(tok_count, dtype=jnp.int32)

    def one_block(first):
        query_blk = lax.dynamic_slice_in_dim(queries, first, block_rows, 0)
        query_pos = first + jnp.arange(block_rows, dtype=jnp.int32)
        query_seg = lax.dynamic_slice_in_dim(segment, first, block_rows, 0)
        scores = (
            jnp.einsum("qhd,khd->hqk", query_blk, keys_all, preferred_element_type=jnp.float32)
            * factor
        )
        allowed = (query_seg[:, None] == segment[None, :]) & (
            key_pos[None, :] <= query_pos[:, None]
        )
        scores = jnp.where(allowed[None], scores, -1e30)
        highest = jnp.max(scores, axis=2, keepdims=True)
        exponent = jnp.exp(scores - highest)
        weights = (exponent / jnp.sum(exponent, axis=2, keepdims=True)).astype(jnp.bfloat16)
        return jnp.einsum(
            "hqk,khd->qhd", weights, values_all, preferred_element_type=jnp.float32
        ).astype(jnp.bfloat16)

    starts = jnp.arange(tok_count // block_rows, dtype=jnp.int32) * block_rows
    blocks = lax.map(one_block, starts)
    return blocks.reshape(tok_count, queries.shape[1] * queries.shape[2])


def ring_gather(block, axis, count, place, index):
    me = lax.axis_index(axis)
    ring, side = place(me)
    half = block.shape[0] // 2

    def send(value, step):
        perm = []
        for i in range(count):
            pos, sd = place(i)
            perm.append((i, index(pos + step, sd, i)))
        return lax.ppermute(value, axis, perm)

    def flip(value):
        perm = []
        for i in range(count):
            pos, sd = place(i)
            perm.append((i, index(pos, 1 - sd, i)))
        return lax.ppermute(value, axis, perm)

    from_minus = send(block, 1)
    from_plus = send(block, -1)
    from_y = flip(block)
    got_minus = send(jnp.concatenate([from_minus[:half], from_y]), 1)
    got_plus = send(jnp.concatenate([from_plus[half:], from_y]), -1)
    last_minus = send(got_minus[half : half + half], 1)
    last_plus = send(got_plus[half + half :], -1)
    pieces = [
        block,
        from_minus,
        from_plus,
        from_y,
        jnp.concatenate([got_minus[:half], got_plus[:half]]),
        got_minus[half:],
        got_plus[half:],
        jnp.concatenate([last_minus, last_plus]),
    ]
    sources = [
        index(ring, side, me),
        index(ring - 1, side, me),
        index(ring + 1, side, me),
        index(ring, 1 - side, me),
        index(ring + 2, side, me),
        index(ring - 1, 1 - side, me),
        index(ring + 1, 1 - side, me),
        index(ring + 2, 1 - side, me),
    ]
    return pieces, sources


def gather_rows(block, row_count):
    pieces, sources = ring_gather(
        block,
        "row",
        row_count,
        lambda r: (r // 2, r % 2),
        lambda pos, sd, r: (pos % 4) * 2 + sd,
    )
    return jnp.stack(pieces), jnp.argsort(jnp.stack(sources))


def scatter_sum(partial, col_count):
    col = lax.axis_index("col")
    chips = col_count // 2
    core = col % 2
    chip = col // 2
    blocks = partial.reshape(chips, 2, -1, partial.shape[1])
    keep = lax.dynamic_index_in_dim(blocks, core, 1, keepdims=False)
    give = lax.dynamic_index_in_dim(blocks, 1 - core, 1, keepdims=False)
    got = lax.ppermute(give.astype(jnp.bfloat16), "col", [(c, c ^ 1) for c in range(col_count)])
    half = keep + got.astype(jnp.float32)
    z_count = chips // 2
    z, y = chip % z_count, chip // z_count
    rows = half.shape[1] // 2

    def dest(dz, dy):
        return [
            (c, ((((c // 2) // z_count) ^ dy) * z_count + ((c // 2) % z_count + dz) % z_count) * 2 + c % 2)
            for c in range(col_count)
        ]

    theirs = lax.dynamic_slice_in_dim(half, (1 - y) * z_count, z_count, 0).astype(jnp.bfloat16)
    side = lax.dynamic_slice_in_dim(half, y * z_count, z_count, 0)
    side = side + lax.ppermute(theirs, "col", dest(0, 1)).astype(jnp.float32)

    def pick(dz):
        return lax.dynamic_index_in_dim(side, (z + dz) % z_count, 0, keepdims=False)

    far = pick(2)
    near_minus = lax.ppermute(far[:rows].astype(jnp.bfloat16), "col", dest(1, 0)).astype(jnp.float32)
    near_plus = lax.ppermute(far[rows:].astype(jnp.bfloat16), "col", dest(-1, 0)).astype(jnp.float32)
    up = pick(1) + jnp.concatenate([near_minus, jnp.zeros_like(near_plus)])
    down = pick(-1) + jnp.concatenate([jnp.zeros_like(near_minus), near_plus])
    total = pick(0)
    total = total + lax.ppermute(up.astype(jnp.bfloat16), "col", dest(1, 0)).astype(jnp.float32)
    total = total + lax.ppermute(down.astype(jnp.bfloat16), "col", dest(-1, 0)).astype(jnp.float32)
    return total.astype(jnp.bfloat16)


def chip_offsets(chips, dy, dz):
    z_count = chips // 2

    def move(cc):
        return ((cc // z_count) ^ dy) * z_count + (cc % z_count + dz) % z_count

    return move


def gather_cols(block, col_count):
    core = lax.axis_index("col") % 2
    pieces, sources = ring_gather(
        block,
        "col",
        col_count,
        lambda c: ((c // 2) % 4, (c // 2) // 4),
        lambda pos, sd, c: (sd * 4 + pos % 4) * 2 + c % 2,
    )
    swap = [(c, c ^ 1) for c in range(col_count)]
    mates = [lax.ppermute(piece, "col", swap) for piece in pieces]
    chips = jnp.stack(sources) // 2
    holder = jnp.concatenate([chips * 2 + core, chips * 2 + 1 - core])
    return jnp.concatenate(pieces + mates, axis=1), holder


def on_device(
    inputs,
    norm_gain,
    query_train,
    key_train,
    value_train,
    out_train,
    adapter_down,
    adapter_up,
    lengths,
):
    col_count = lax.axis_size("col")
    row_count = lax.axis_size("row")
    local_rows = query_train.shape[0]
    head_local = HEADS // col_count
    merged_width = 3 * head_local * HS
    trained = jnp.stack(
        (query_train.astype(jnp.bfloat16), key_train.astype(jnp.bfloat16), value_train.astype(jnp.bfloat16)),
        axis=1,
    ).reshape(local_rows, 3, col_count, head_local * HS)
    trained = jnp.transpose(trained, (2, 0, 1, 3))
    moved = lax.all_to_all(trained, "col", 0, 0, tiled=True)
    moved = moved.reshape(col_count * local_rows, merged_width)
    moved, inputs = lax.optimization_barrier((moved, inputs))
    stacked, slot = gather_rows(moved, row_count)
    whole, holder = gather_cols(inputs, col_count)
    block_count = holder.shape[0]
    tok_count = whole.shape[0]
    gain = jnp.take(norm_gain.reshape(block_count, -1), holder, axis=0).reshape(-1)
    down = jnp.take(
        adapter_down.reshape(block_count, -1, adapter_down.shape[1]), holder, axis=0
    ).reshape(-1, adapter_down.shape[1])
    normed = normalize(whole, gain)
    adapted = jnp.dot(normed, down, preferred_element_type=jnp.float32).astype(jnp.bfloat16)
    per_row = block_count // row_count
    blocks = stacked.reshape(row_count * per_row, -1, merged_width)
    picked = jnp.take(slot, holder // per_row) * per_row + holder % per_row
    merged = jnp.take(blocks, picked, axis=0).reshape(-1, merged_width)
    product = jnp.dot(normed, merged, preferred_element_type=jnp.float32)
    up_columns = adapter_up.reshape(adapter_up.shape[0], merged_width)
    joined = (product + jnp.dot(adapted, up_columns, preferred_element_type=jnp.float32)).astype(
        jnp.bfloat16
    )
    joined = joined.reshape(tok_count, 3, head_local, HS)
    segment = segment_of(lengths[0], tok_count)
    attended = attend(joined[:, 0], joined[:, 1], joined[:, 2], segment)
    out_local = out_train.astype(jnp.bfloat16)
    out_cols = out_local.shape[1]
    out_sent = out_local.reshape(col_count, head_local * HS, out_cols)
    out_sent = jnp.broadcast_to(out_sent[None], (row_count,) + out_sent.shape).reshape(
        row_count * col_count, head_local * HS, out_cols
    )
    out_block = lax.all_to_all(out_sent, ("row", "col"), 0, 0, tiled=True)
    out_block = jnp.transpose(out_block, (1, 0, 2)).reshape(head_local * HS, -1)
    partial_out = jnp.dot(attended, out_block, preferred_element_type=jnp.float32)
    return scatter_sum(partial_out, col_count)


def solution(mesh):
    in_specs = (
        P("row", "col"),
        P(),
        P(("row", "col"), None),
        P(("row", "col"), None),
        P(("row", "col"), None),
        P(None, ("row", "col")),
        P(),
        P(None, None, "col", None),
        P("row", None),
    )
    out_specs = P(("row", "col"), None)
    return jax.shard_map(
        on_device, mesh=mesh, in_specs=in_specs, out_specs=out_specs, check_vma=False
    )
```

```python
import math

import jax
import jax.numpy as jnp
from jax import lax
from jax.sharding import PartitionSpec as P

HEADS = 32
HS = 128


def normalize(whole, norm_gain):
    floats = whole.astype(jnp.float32)
    mean_square = jnp.mean(floats * floats, axis=1, keepdims=True)
    return (floats * lax.rsqrt(mean_square + 1e-05) * norm_gain).astype(jnp.bfloat16)


def segment_of(lengths_row, tok_count):
    position = jnp.arange(tok_count, dtype=jnp.int32)
    prompt_ends = jnp.cumsum(lengths_row)
    return jnp.sum((position[:, None] >= prompt_ends[None, :]).astype(jnp.int32), axis=1)


def attend(queries, keys_all, values_all, segment):
    tok_count = queries.shape[0]
    block_rows = min(512, tok_count)
    factor = 1.0 / math.sqrt(queries.shape[2])
    key_pos = jnp.arange(tok_count, dtype=jnp.int32)

    def one_block(first):
        query_blk = lax.dynamic_slice_in_dim(queries, first, block_rows, 0)
        query_pos = first + jnp.arange(block_rows, dtype=jnp.int32)
        query_seg = lax.dynamic_slice_in_dim(segment, first, block_rows, 0)
        scores = (
            jnp.einsum("qhd,khd->hqk", query_blk, keys_all, preferred_element_type=jnp.float32)
            * factor
        )
        allowed = (query_seg[:, None] == segment[None, :]) & (
            key_pos[None, :] <= query_pos[:, None]
        )
        scores = jnp.where(allowed[None], scores, -1e30)
        highest = jnp.max(scores, axis=2, keepdims=True)
        exponent = jnp.exp(scores - highest)
        weights = (exponent / jnp.sum(exponent, axis=2, keepdims=True)).astype(jnp.bfloat16)
        return jnp.einsum(
            "hqk,khd->qhd", weights, values_all, preferred_element_type=jnp.float32
        ).astype(jnp.bfloat16)

    starts = jnp.arange(tok_count // block_rows, dtype=jnp.int32) * block_rows
    blocks = lax.map(one_block, starts)
    return blocks.reshape(tok_count, queries.shape[1] * queries.shape[2])


def attend_rows(query_blk, query_pos, query_seg, keys_all, values_all, segment):
    factor = 1.0 / math.sqrt(query_blk.shape[2])
    key_pos = jnp.arange(keys_all.shape[0], dtype=jnp.int32)
    scores = (
        jnp.einsum("qhd,khd->hqk", query_blk, keys_all, preferred_element_type=jnp.float32)
        * factor
    )
    allowed = (query_seg[:, None] == segment[None, :]) & (key_pos[None, :] <= query_pos[:, None])
    scores = jnp.where(allowed[None], scores, -1e30)
    highest = jnp.max(scores, axis=2, keepdims=True)
    exponent = jnp.exp(scores - highest)
    weights = (exponent / jnp.sum(exponent, axis=2, keepdims=True)).astype(jnp.bfloat16)
    return jnp.einsum(
        "hqk,khd->qhd", weights, values_all, preferred_element_type=jnp.float32
    ).astype(jnp.bfloat16)


def ring_gather(block, axis, count, place, index):
    me = lax.axis_index(axis)
    ring, side = place(me)
    half = block.shape[0] // 2

    def send(value, step):
        perm = []
        for i in range(count):
            pos, sd = place(i)
            perm.append((i, index(pos + step, sd, i)))
        return lax.ppermute(value, axis, perm)

    def flip(value):
        perm = []
        for i in range(count):
            pos, sd = place(i)
            perm.append((i, index(pos, 1 - sd, i)))
        return lax.ppermute(value, axis, perm)

    from_minus = send(block, 1)
    from_plus = send(block, -1)
    from_y = flip(block)
    got_minus = send(jnp.concatenate([from_minus[:half], from_y]), 1)
    got_plus = send(jnp.concatenate([from_plus[half:], from_y]), -1)
    last_minus = send(got_minus[half : half + half], 1)
    last_plus = send(got_plus[half + half :], -1)
    pieces = [
        block,
        from_minus,
        from_plus,
        from_y,
        jnp.concatenate([got_minus[:half], got_plus[:half]]),
        got_minus[half:],
        got_plus[half:],
        jnp.concatenate([last_minus, last_plus]),
    ]
    sources = [
        index(ring, side, me),
        index(ring - 1, side, me),
        index(ring + 1, side, me),
        index(ring, 1 - side, me),
        index(ring + 2, side, me),
        index(ring - 1, 1 - side, me),
        index(ring + 1, 1 - side, me),
        index(ring + 2, 1 - side, me),
    ]
    return pieces, sources


def gather_rows(block, row_count):
    pieces, sources = ring_gather(
        block,
        "row",
        row_count,
        lambda r: (r // 2, r % 2),
        lambda pos, sd, r: (pos % 4) * 2 + sd,
    )
    return jnp.stack(pieces), jnp.argsort(jnp.stack(sources))


def scatter_sum(partial, col_count):
    col = lax.axis_index("col")
    chips = col_count // 2
    core = col % 2
    chip = col // 2
    blocks = partial.reshape(chips, 2, -1, partial.shape[1])
    keep = lax.dynamic_index_in_dim(blocks, core, 1, keepdims=False)
    give = lax.dynamic_index_in_dim(blocks, 1 - core, 1, keepdims=False)
    got = lax.ppermute(give.astype(jnp.bfloat16), "col", [(c, c ^ 1) for c in range(col_count)])
    half = keep + got.astype(jnp.float32)
    z_count = chips // 2
    total = lax.dynamic_index_in_dim(half, chip, 0, keepdims=False)
    for dz in range(z_count):
        for dy in range(2):
            if dz == 0 and dy == 0:
                continue
            def dest(c):
                cc = c // 2
                return (((cc // z_count) ^ dy) * z_count + (cc % z_count + dz) % z_count) * 2 + c % 2
            perm = [(c, dest(c)) for c in range(col_count)]
            target = ((chip // z_count) ^ dy) * z_count + (chip % z_count + dz) % z_count
            sent = lax.dynamic_index_in_dim(half, target, 0, keepdims=False).astype(jnp.bfloat16)
            total = total + lax.ppermute(sent, "col", perm).astype(jnp.float32)
    return total.astype(jnp.bfloat16)


def chip_offsets(chips, dy, dz):
    z_count = chips // 2

    def move(cc):
        return ((cc // z_count) ^ dy) * z_count + (cc % z_count + dz) % z_count

    return move


def gather_cols(block, col_count):
    core = lax.axis_index("col") % 2
    pieces, sources = ring_gather(
        block,
        "col",
        col_count,
        lambda c: ((c // 2) % 4, (c // 2) // 4),
        lambda pos, sd, c: (sd * 4 + pos % 4) * 2 + c % 2,
    )
    swap = [(c, c ^ 1) for c in range(col_count)]
    mates = [lax.ppermute(piece, "col", swap) for piece in pieces]
    chips = jnp.stack(sources) // 2
    holder = jnp.concatenate([chips * 2 + core, chips * 2 + 1 - core])
    return jnp.concatenate(pieces + mates, axis=1), holder


def on_device(
    inputs,
    norm_gain,
    query_train,
    key_train,
    value_train,
    out_train,
    adapter_down,
    adapter_up,
    lengths,
):
    col_count = lax.axis_size("col")
    row_count = lax.axis_size("row")
    local_rows = query_train.shape[0]
    head_local = HEADS // col_count
    merged_width = 3 * head_local * HS
    trained = jnp.stack(
        (query_train.astype(jnp.bfloat16), key_train.astype(jnp.bfloat16), value_train.astype(jnp.bfloat16)),
        axis=1,
    ).reshape(local_rows, 3, col_count, head_local * HS)
    trained = jnp.transpose(trained, (2, 0, 1, 3))
    moved = lax.all_to_all(trained, "col", 0, 0, tiled=True)
    moved = moved.reshape(col_count * local_rows, merged_width)
    moved, inputs = lax.optimization_barrier((moved, inputs))
    stacked, slot = gather_rows(moved, row_count)
    whole, holder = gather_cols(inputs, col_count)
    block_count = holder.shape[0]
    tok_count = whole.shape[0]
    gain = jnp.take(norm_gain.reshape(block_count, -1), holder, axis=0).reshape(-1)
    down = jnp.take(
        adapter_down.reshape(block_count, -1, adapter_down.shape[1]), holder, axis=0
    ).reshape(-1, adapter_down.shape[1])
    normed = normalize(whole, gain)
    adapted = jnp.dot(normed, down, preferred_element_type=jnp.float32).astype(jnp.bfloat16)
    per_row = block_count // row_count
    blocks = stacked.reshape(row_count * per_row, -1, merged_width)
    picked = jnp.take(slot, holder // per_row) * per_row + holder % per_row
    merged = jnp.take(blocks, picked, axis=0).reshape(-1, merged_width)
    product = jnp.dot(normed, merged, preferred_element_type=jnp.float32)
    up_columns = adapter_up.reshape(adapter_up.shape[0], merged_width)
    joined = (product + jnp.dot(adapted, up_columns, preferred_element_type=jnp.float32)).astype(
        jnp.bfloat16
    )
    joined = joined.reshape(tok_count, 3, head_local, HS)
    segment = segment_of(lengths[0], tok_count)
    out_local = out_train.astype(jnp.bfloat16)
    out_cols = out_local.shape[1]
    out_sent = out_local.reshape(col_count, head_local * HS, out_cols)
    out_sent = jnp.broadcast_to(out_sent[None], (row_count,) + out_sent.shape).reshape(
        row_count * col_count, head_local * HS, out_cols
    )
    out_block = lax.all_to_all(out_sent, ("row", "col"), 0, 0, tiled=True)
    out_block = jnp.transpose(out_block, (1, 0, 2)).reshape(head_local * HS, -1)
    chunks = 2
    part_rows = tok_count // col_count // chunks
    position = jnp.arange(tok_count, dtype=jnp.int32)
    results = []
    for j in range(chunks):
        def pick(a):
            return a.reshape((col_count, chunks, part_rows) + a.shape[1:])[:, j].reshape(
                (-1,) + a.shape[1:]
            )

        attended = attend_rows(
            pick(joined[:, 0]), pick(position), pick(segment), joined[:, 1], joined[:, 2], segment
        )
        attended = attended.reshape(attended.shape[0], -1)
        partial_out = jnp.dot(attended, out_block, preferred_element_type=jnp.float32)
        results.append(scatter_sum(partial_out, col_count))
    return jnp.concatenate(results, axis=0)


def solution(mesh):
    in_specs = (
        P("row", "col"),
        P(),
        P(("row", "col"), None),
        P(("row", "col"), None),
        P(("row", "col"), None),
        P(None, ("row", "col")),
        P(),
        P(None, None, "col", None),
        P("row", None),
    )
    out_specs = P(("row", "col"), None)
    return jax.shard_map(
        on_device, mesh=mesh, in_specs=in_specs, out_specs=out_specs, check_vma=False
    )
```

```python
import math

import jax
import jax.numpy as jnp
from jax import lax
from jax.sharding import PartitionSpec as P

HEADS = 32
HS = 128


def normalize(whole, norm_gain):
    floats = whole.astype(jnp.float32)
    mean_square = jnp.mean(floats * floats, axis=1, keepdims=True)
    return (floats * lax.rsqrt(mean_square + 1e-05) * norm_gain).astype(jnp.bfloat16)


def segment_of(lengths_row, tok_count):
    position = jnp.arange(tok_count, dtype=jnp.int32)
    prompt_ends = jnp.cumsum(lengths_row)
    return jnp.sum((position[:, None] >= prompt_ends[None, :]).astype(jnp.int32), axis=1)


def attend(queries, keys_all, values_all, segment):
    tok_count = queries.shape[0]
    block_rows = min(512, tok_count)
    factor = 1.0 / math.sqrt(queries.shape[2])
    key_pos = jnp.arange(tok_count, dtype=jnp.int32)

    def one_block(first):
        query_blk = lax.dynamic_slice_in_dim(queries, first, block_rows, 0)
        query_pos = first + jnp.arange(block_rows, dtype=jnp.int32)
        query_seg = lax.dynamic_slice_in_dim(segment, first, block_rows, 0)
        scores = (
            jnp.einsum("qhd,khd->hqk", query_blk, keys_all, preferred_element_type=jnp.float32)
            * factor
        )
        allowed = (query_seg[:, None] == segment[None, :]) & (
            key_pos[None, :] <= query_pos[:, None]
        )
        scores = jnp.where(allowed[None], scores, -1e30)
        highest = jnp.max(scores, axis=2, keepdims=True)
        exponent = jnp.exp(scores - highest)
        weights = (exponent / jnp.sum(exponent, axis=2, keepdims=True)).astype(jnp.bfloat16)
        return jnp.einsum(
            "hqk,khd->qhd", weights, values_all, preferred_element_type=jnp.float32
        ).astype(jnp.bfloat16)

    starts = jnp.arange(tok_count // block_rows, dtype=jnp.int32) * block_rows
    blocks = lax.map(one_block, starts)
    return blocks.reshape(tok_count, queries.shape[1] * queries.shape[2])


def attend_rows(query_blk, query_pos, query_seg, keys_all, values_all, segment):
    factor = 1.0 / math.sqrt(query_blk.shape[2])
    key_pos = jnp.arange(keys_all.shape[0], dtype=jnp.int32)
    scores = (
        jnp.einsum("qhd,khd->hqk", query_blk, keys_all, preferred_element_type=jnp.float32)
        * factor
    )
    allowed = (query_seg[:, None] == segment[None, :]) & (key_pos[None, :] <= query_pos[:, None])
    scores = jnp.where(allowed[None], scores, -1e30)
    highest = jnp.max(scores, axis=2, keepdims=True)
    exponent = jnp.exp(scores - highest)
    weights = (exponent / jnp.sum(exponent, axis=2, keepdims=True)).astype(jnp.bfloat16)
    return jnp.einsum(
        "hqk,khd->qhd", weights, values_all, preferred_element_type=jnp.float32
    ).astype(jnp.bfloat16)


def ring_gather(block, axis, count, place, index):
    me = lax.axis_index(axis)
    ring, side = place(me)
    half = block.shape[0] // 2

    def send(value, step):
        perm = []
        for i in range(count):
            pos, sd = place(i)
            perm.append((i, index(pos + step, sd, i)))
        return lax.ppermute(value, axis, perm)

    def flip(value):
        perm = []
        for i in range(count):
            pos, sd = place(i)
            perm.append((i, index(pos, 1 - sd, i)))
        return lax.ppermute(value, axis, perm)

    from_minus = send(block, 1)
    from_plus = send(block, -1)
    from_y = flip(block)
    got_minus = send(jnp.concatenate([from_minus[:half], from_y]), 1)
    got_plus = send(jnp.concatenate([from_plus[half:], from_y]), -1)
    last_minus = send(got_minus[half : half + half], 1)
    last_plus = send(got_plus[half + half :], -1)
    pieces = [
        block,
        from_minus,
        from_plus,
        from_y,
        jnp.concatenate([got_minus[:half], got_plus[:half]]),
        got_minus[half:],
        got_plus[half:],
        jnp.concatenate([last_minus, last_plus]),
    ]
    sources = [
        index(ring, side, me),
        index(ring - 1, side, me),
        index(ring + 1, side, me),
        index(ring, 1 - side, me),
        index(ring + 2, side, me),
        index(ring - 1, 1 - side, me),
        index(ring + 1, 1 - side, me),
        index(ring + 2, 1 - side, me),
    ]
    return pieces, sources


def gather_rows(block, row_count):
    pieces, sources = ring_gather(
        block,
        "row",
        row_count,
        lambda r: (r // 2, r % 2),
        lambda pos, sd, r: (pos % 4) * 2 + sd,
    )
    return jnp.stack(pieces), jnp.argsort(jnp.stack(sources))


def scatter_sum(partial, col_count):
    col = lax.axis_index("col")
    chips = col_count // 2
    core = col % 2
    chip = col // 2
    blocks = partial.reshape(chips, 2, -1, partial.shape[1])
    keep = lax.dynamic_index_in_dim(blocks, core, 1, keepdims=False)
    give = lax.dynamic_index_in_dim(blocks, 1 - core, 1, keepdims=False)
    got = lax.ppermute(give.astype(jnp.bfloat16), "col", [(c, c ^ 1) for c in range(col_count)])
    half = keep + got.astype(jnp.float32)
    z_count = chips // 2
    total = lax.dynamic_index_in_dim(half, chip, 0, keepdims=False)
    for dz in range(z_count):
        for dy in range(2):
            if dz == 0 and dy == 0:
                continue
            def dest(c):
                cc = c // 2
                return (((cc // z_count) ^ dy) * z_count + (cc % z_count + dz) % z_count) * 2 + c % 2
            perm = [(c, dest(c)) for c in range(col_count)]
            target = ((chip // z_count) ^ dy) * z_count + (chip % z_count + dz) % z_count
            sent = lax.dynamic_index_in_dim(half, target, 0, keepdims=False).astype(jnp.bfloat16)
            total = total + lax.ppermute(sent, "col", perm).astype(jnp.float32)
    return total.astype(jnp.bfloat16)


def chip_offsets(chips, dy, dz):
    z_count = chips // 2

    def move(cc):
        return ((cc // z_count) ^ dy) * z_count + (cc % z_count + dz) % z_count

    return move


def gather_cols(block, col_count):
    core = lax.axis_index("col") % 2
    pieces, sources = ring_gather(
        block,
        "col",
        col_count,
        lambda c: ((c // 2) % 4, (c // 2) // 4),
        lambda pos, sd, c: (sd * 4 + pos % 4) * 2 + c % 2,
    )
    swap = [(c, c ^ 1) for c in range(col_count)]
    mates = [lax.ppermute(piece, "col", swap) for piece in pieces]
    chips = jnp.stack(sources) // 2
    holder = jnp.concatenate([chips * 2 + core, chips * 2 + 1 - core])
    return jnp.concatenate(pieces + mates, axis=1), holder


def on_device(
    inputs,
    norm_gain,
    query_train,
    key_train,
    value_train,
    out_train,
    adapter_down,
    adapter_up,
    lengths,
):
    col_count = lax.axis_size("col")
    row_count = lax.axis_size("row")
    local_rows = query_train.shape[0]
    head_local = HEADS // col_count
    merged_width = 3 * head_local * HS
    trained = jnp.stack(
        (query_train.astype(jnp.bfloat16), key_train.astype(jnp.bfloat16), value_train.astype(jnp.bfloat16)),
        axis=1,
    ).reshape(local_rows, 3, col_count, head_local * HS)
    trained = jnp.transpose(trained, (2, 0, 1, 3))
    moved = lax.all_to_all(trained, "col", 0, 0, tiled=True)
    moved = moved.reshape(col_count * local_rows, merged_width)
    stacked, slot = gather_rows(moved, row_count)
    whole, holder = gather_cols(inputs, col_count)
    block_count = holder.shape[0]
    tok_count = whole.shape[0]
    gain = jnp.take(norm_gain.reshape(block_count, -1), holder, axis=0).reshape(-1)
    down = jnp.take(
        adapter_down.reshape(block_count, -1, adapter_down.shape[1]), holder, axis=0
    ).reshape(-1, adapter_down.shape[1])
    normed = normalize(whole, gain)
    adapted = jnp.dot(normed, down, preferred_element_type=jnp.float32).astype(jnp.bfloat16)
    per_row = block_count // row_count
    blocks = stacked.reshape(row_count * per_row, -1, merged_width)
    picked = jnp.take(slot, holder // per_row) * per_row + holder % per_row
    merged = jnp.take(blocks, picked, axis=0).reshape(-1, merged_width)
    product = jnp.dot(normed, merged, preferred_element_type=jnp.float32)
    up_columns = adapter_up.reshape(adapter_up.shape[0], merged_width)
    joined = (product + jnp.dot(adapted, up_columns, preferred_element_type=jnp.float32)).astype(
        jnp.bfloat16
    )
    joined = joined.reshape(tok_count, 3, head_local, HS)
    segment = segment_of(lengths[0], tok_count)
    out_local = out_train.astype(jnp.bfloat16)
    out_cols = out_local.shape[1]
    out_sent = out_local.reshape(col_count, head_local * HS, out_cols)
    out_sent = jnp.broadcast_to(out_sent[None], (row_count,) + out_sent.shape).reshape(
        row_count * col_count, head_local * HS, out_cols
    )
    out_block = lax.all_to_all(out_sent, ("row", "col"), 0, 0, tiled=True)
    out_block = jnp.transpose(out_block, (1, 0, 2)).reshape(head_local * HS, -1)
    chunks = 2
    part_rows = tok_count // col_count // chunks
    position = jnp.arange(tok_count, dtype=jnp.int32)
    results = []
    for j in range(chunks):
        def pick(a):
            return a.reshape((col_count, chunks, part_rows) + a.shape[1:])[:, j].reshape(
                (-1,) + a.shape[1:]
            )

        attended = attend_rows(
            pick(joined[:, 0]), pick(position), pick(segment), joined[:, 1], joined[:, 2], segment
        )
        attended = attended.reshape(attended.shape[0], -1)
        partial_out = jnp.dot(attended, out_block, preferred_element_type=jnp.float32)
        results.append(scatter_sum(partial_out, col_count))
    return jnp.concatenate(results, axis=0)


def solution(mesh):
    in_specs = (
        P("row", "col"),
        P(),
        P(("row", "col"), None),
        P(("row", "col"), None),
        P(("row", "col"), None),
        P(None, ("row", "col")),
        P(),
        P(None, None, "col", None),
        P("row", None),
    )
    out_specs = P(("row", "col"), None)
    return jax.shard_map(
        on_device, mesh=mesh, in_specs=in_specs, out_specs=out_specs, check_vma=False
    )
```

```python
import math

import jax
import jax.numpy as jnp
from jax import lax
from jax.sharding import PartitionSpec as P

HEADS = 32
HS = 128


def normalize(whole, norm_gain):
    floats = whole.astype(jnp.float32)
    mean_square = jnp.mean(floats * floats, axis=1, keepdims=True)
    return (floats * lax.rsqrt(mean_square + 1e-05) * norm_gain).astype(jnp.bfloat16)


def segment_of(lengths_row, tok_count):
    position = jnp.arange(tok_count, dtype=jnp.int32)
    prompt_ends = jnp.cumsum(lengths_row)
    return jnp.sum((position[:, None] >= prompt_ends[None, :]).astype(jnp.int32), axis=1)


def attend(queries, keys_all, values_all, segment):
    tok_count = queries.shape[0]
    block_rows = min(512, tok_count)
    factor = 1.0 / math.sqrt(queries.shape[2])
    key_pos = jnp.arange(tok_count, dtype=jnp.int32)

    def one_block(first):
        query_blk = lax.dynamic_slice_in_dim(queries, first, block_rows, 0)
        query_pos = first + jnp.arange(block_rows, dtype=jnp.int32)
        query_seg = lax.dynamic_slice_in_dim(segment, first, block_rows, 0)
        scores = (
            jnp.einsum("qhd,khd->hqk", query_blk, keys_all, preferred_element_type=jnp.float32)
            * factor
        )
        allowed = (query_seg[:, None] == segment[None, :]) & (
            key_pos[None, :] <= query_pos[:, None]
        )
        scores = jnp.where(allowed[None], scores, -1e30)
        highest = jnp.max(scores, axis=2, keepdims=True)
        exponent = jnp.exp(scores - highest)
        weights = (exponent / jnp.sum(exponent, axis=2, keepdims=True)).astype(jnp.bfloat16)
        return jnp.einsum(
            "hqk,khd->qhd", weights, values_all, preferred_element_type=jnp.float32
        ).astype(jnp.bfloat16)

    starts = jnp.arange(tok_count // block_rows, dtype=jnp.int32) * block_rows
    blocks = lax.map(one_block, starts)
    return blocks.reshape(tok_count, queries.shape[1] * queries.shape[2])


def attend_rows(query_blk, query_pos, query_seg, keys_all, values_all, segment):
    factor = 1.0 / math.sqrt(query_blk.shape[2])
    key_pos = jnp.arange(keys_all.shape[0], dtype=jnp.int32)
    scores = (
        jnp.einsum("qhd,khd->hqk", query_blk, keys_all, preferred_element_type=jnp.float32)
        * factor
    )
    allowed = (query_seg[:, None] == segment[None, :]) & (key_pos[None, :] <= query_pos[:, None])
    scores = jnp.where(allowed[None], scores, -1e30)
    highest = jnp.max(scores, axis=2, keepdims=True)
    exponent = jnp.exp(scores - highest)
    weights = (exponent / jnp.sum(exponent, axis=2, keepdims=True)).astype(jnp.bfloat16)
    return jnp.einsum(
        "hqk,khd->qhd", weights, values_all, preferred_element_type=jnp.float32
    ).astype(jnp.bfloat16)


def ring_gather(block, axis, count, place, index):
    me = lax.axis_index(axis)
    ring, side = place(me)
    half = block.shape[0] // 2

    def send(value, step):
        perm = []
        for i in range(count):
            pos, sd = place(i)
            perm.append((i, index(pos + step, sd, i)))
        return lax.ppermute(value, axis, perm)

    def flip(value):
        perm = []
        for i in range(count):
            pos, sd = place(i)
            perm.append((i, index(pos, 1 - sd, i)))
        return lax.ppermute(value, axis, perm)

    from_minus = send(block, 1)
    from_plus = send(block, -1)
    from_y = flip(block)
    got_minus = send(jnp.concatenate([from_minus[:half], from_y]), 1)
    got_plus = send(jnp.concatenate([from_plus[half:], from_y]), -1)
    last_minus = send(got_minus[half : half + half], 1)
    last_plus = send(got_plus[half + half :], -1)
    pieces = [
        block,
        from_minus,
        from_plus,
        from_y,
        jnp.concatenate([got_minus[:half], got_plus[:half]]),
        got_minus[half:],
        got_plus[half:],
        jnp.concatenate([last_minus, last_plus]),
    ]
    sources = [
        index(ring, side, me),
        index(ring - 1, side, me),
        index(ring + 1, side, me),
        index(ring, 1 - side, me),
        index(ring + 2, side, me),
        index(ring - 1, 1 - side, me),
        index(ring + 1, 1 - side, me),
        index(ring + 2, 1 - side, me),
    ]
    return pieces, sources


def gather_rows(block, row_count):
    pieces, sources = ring_gather(
        block,
        "row",
        row_count,
        lambda r: (r // 2, r % 2),
        lambda pos, sd, r: (pos % 4) * 2 + sd,
    )
    return jnp.stack(pieces), jnp.argsort(jnp.stack(sources))


def scatter_sum(partial, col_count):
    col = lax.axis_index("col")
    chips = col_count // 2
    core = col % 2
    chip = col // 2
    blocks = partial.reshape(chips, 2, -1, partial.shape[1])
    keep = lax.dynamic_index_in_dim(blocks, core, 1, keepdims=False)
    give = lax.dynamic_index_in_dim(blocks, 1 - core, 1, keepdims=False)
    got = lax.ppermute(give.astype(jnp.bfloat16), "col", [(c, c ^ 1) for c in range(col_count)])
    half = keep + got.astype(jnp.float32)
    z_count = chips // 2
    total = lax.dynamic_index_in_dim(half, chip, 0, keepdims=False)
    for dz in range(z_count):
        for dy in range(2):
            if dz == 0 and dy == 0:
                continue
            def dest(c):
                cc = c // 2
                return (((cc // z_count) ^ dy) * z_count + (cc % z_count + dz) % z_count) * 2 + c % 2
            perm = [(c, dest(c)) for c in range(col_count)]
            target = ((chip // z_count) ^ dy) * z_count + (chip % z_count + dz) % z_count
            sent = lax.dynamic_index_in_dim(half, target, 0, keepdims=False).astype(jnp.bfloat16)
            total = total + lax.ppermute(sent, "col", perm).astype(jnp.float32)
    return total.astype(jnp.bfloat16)


def chip_offsets(chips, dy, dz):
    z_count = chips // 2

    def move(cc):
        return ((cc // z_count) ^ dy) * z_count + (cc % z_count + dz) % z_count

    return move


def gather_cols(block, col_count):
    core = lax.axis_index("col") % 2
    pieces, sources = ring_gather(
        block,
        "col",
        col_count,
        lambda c: ((c // 2) % 4, (c // 2) // 4),
        lambda pos, sd, c: (sd * 4 + pos % 4) * 2 + c % 2,
    )
    swap = [(c, c ^ 1) for c in range(col_count)]
    mates = [lax.ppermute(piece, "col", swap) for piece in pieces]
    chips = jnp.stack(sources) // 2
    holder = jnp.concatenate([chips * 2 + core, chips * 2 + 1 - core])
    return jnp.concatenate(pieces + mates, axis=1), holder


def on_device(
    inputs,
    norm_gain,
    query_train,
    key_train,
    value_train,
    out_train,
    adapter_down,
    adapter_up,
    lengths,
):
    col_count = lax.axis_size("col")
    row_count = lax.axis_size("row")
    local_rows = query_train.shape[0]
    head_local = HEADS // col_count
    merged_width = 3 * head_local * HS
    trained = jnp.stack(
        (query_train.astype(jnp.bfloat16), key_train.astype(jnp.bfloat16), value_train.astype(jnp.bfloat16)),
        axis=1,
    ).reshape(local_rows, 3, col_count, head_local * HS)
    trained = jnp.transpose(trained, (2, 0, 1, 3))
    moved = lax.all_to_all(trained, "col", 0, 0, tiled=True)
    moved = moved.reshape(col_count * local_rows, merged_width)
    stacked, slot = gather_rows(moved, row_count)
    whole, holder = gather_cols(inputs, col_count)
    block_count = holder.shape[0]
    tok_count = whole.shape[0]
    gain = jnp.take(norm_gain.reshape(block_count, -1), holder, axis=0).reshape(-1)
    down = jnp.take(
        adapter_down.reshape(block_count, -1, adapter_down.shape[1]), holder, axis=0
    ).reshape(-1, adapter_down.shape[1])
    normed = normalize(whole, gain)
    adapted = jnp.dot(normed, down, preferred_element_type=jnp.float32).astype(jnp.bfloat16)
    per_row = block_count // row_count
    blocks = stacked.reshape(row_count * per_row, -1, merged_width)
    picked = jnp.take(slot, holder // per_row) * per_row + holder % per_row
    merged = jnp.take(blocks, picked, axis=0).reshape(-1, merged_width)
    product = jnp.dot(normed, merged, preferred_element_type=jnp.float32)
    up_columns = adapter_up.reshape(adapter_up.shape[0], merged_width)
    joined = (product + jnp.dot(adapted, up_columns, preferred_element_type=jnp.float32)).astype(
        jnp.bfloat16
    )
    joined = joined.reshape(tok_count, 3, head_local, HS)
    segment = segment_of(lengths[0], tok_count)
    out_local = out_train.astype(jnp.bfloat16)
    out_cols = out_local.shape[1]
    out_sent = out_local.reshape(col_count, head_local * HS, out_cols)
    out_sent = jnp.broadcast_to(out_sent[None], (row_count,) + out_sent.shape).reshape(
        row_count * col_count, head_local * HS, out_cols
    )
    out_block = lax.all_to_all(out_sent, ("row", "col"), 0, 0, tiled=True)
    out_block = jnp.transpose(out_block, (1, 0, 2)).reshape(head_local * HS, -1)
    chunks = 4
    part_rows = tok_count // col_count // chunks
    position = jnp.arange(tok_count, dtype=jnp.int32)
    results = []
    for j in range(chunks):
        def pick(a):
            return a.reshape((col_count, chunks, part_rows) + a.shape[1:])[:, j].reshape(
                (-1,) + a.shape[1:]
            )

        attended = attend_rows(
            pick(joined[:, 0]), pick(position), pick(segment), joined[:, 1], joined[:, 2], segment
        )
        attended = attended.reshape(attended.shape[0], -1)
        partial_out = jnp.dot(attended, out_block, preferred_element_type=jnp.float32)
        results.append(scatter_sum(partial_out, col_count))
    return jnp.concatenate(results, axis=0)


def solution(mesh):
    in_specs = (
        P("row", "col"),
        P(),
        P(("row", "col"), None),
        P(("row", "col"), None),
        P(("row", "col"), None),
        P(None, ("row", "col")),
        P(),
        P(None, None, "col", None),
        P("row", None),
    )
    out_specs = P(("row", "col"), None)
    return jax.shard_map(
        on_device, mesh=mesh, in_specs=in_specs, out_specs=out_specs, check_vma=False
    )
```

```python
import math

import jax
import jax.numpy as jnp
from jax import lax
from jax.sharding import PartitionSpec as P

HEADS = 32
HS = 128


def normalize(whole, norm_gain):
    floats = whole.astype(jnp.float32)
    mean_square = jnp.mean(floats * floats, axis=1, keepdims=True)
    return (floats * lax.rsqrt(mean_square + 1e-05) * norm_gain).astype(jnp.bfloat16)


def segment_of(lengths_row, tok_count):
    position = jnp.arange(tok_count, dtype=jnp.int32)
    prompt_ends = jnp.cumsum(lengths_row)
    return jnp.sum((position[:, None] >= prompt_ends[None, :]).astype(jnp.int32), axis=1)


def attend(queries, keys_all, values_all, segment):
    tok_count = queries.shape[0]
    block_rows = min(512, tok_count)
    factor = 1.0 / math.sqrt(queries.shape[2])
    key_pos = jnp.arange(tok_count, dtype=jnp.int32)

    def one_block(first):
        query_blk = lax.dynamic_slice_in_dim(queries, first, block_rows, 0)
        query_pos = first + jnp.arange(block_rows, dtype=jnp.int32)
        query_seg = lax.dynamic_slice_in_dim(segment, first, block_rows, 0)
        scores = (
            jnp.einsum("qhd,khd->hqk", query_blk, keys_all, preferred_element_type=jnp.float32)
            * factor
        )
        allowed = (query_seg[:, None] == segment[None, :]) & (
            key_pos[None, :] <= query_pos[:, None]
        )
        scores = jnp.where(allowed[None], scores, -1e30)
        highest = jnp.max(scores, axis=2, keepdims=True)
        exponent = jnp.exp(scores - highest)
        weights = (exponent / jnp.sum(exponent, axis=2, keepdims=True)).astype(jnp.bfloat16)
        return jnp.einsum(
            "hqk,khd->qhd", weights, values_all, preferred_element_type=jnp.float32
        ).astype(jnp.bfloat16)

    starts = jnp.arange(tok_count // block_rows, dtype=jnp.int32) * block_rows
    blocks = lax.map(one_block, starts)
    return blocks.reshape(tok_count, queries.shape[1] * queries.shape[2])


def attend_rows(query_blk, query_pos, query_seg, keys_all, values_all, segment):
    factor = 1.0 / math.sqrt(query_blk.shape[2])
    key_pos = jnp.arange(keys_all.shape[0], dtype=jnp.int32)
    scores = (
        jnp.einsum("qhd,khd->hqk", query_blk, keys_all, preferred_element_type=jnp.float32)
        * factor
    )
    allowed = (query_seg[:, None] == segment[None, :]) & (key_pos[None, :] <= query_pos[:, None])
    scores = jnp.where(allowed[None], scores, -1e30)
    highest = jnp.max(scores, axis=2, keepdims=True)
    exponent = jnp.exp(scores - highest)
    weights = (exponent / jnp.sum(exponent, axis=2, keepdims=True)).astype(jnp.bfloat16)
    return jnp.einsum(
        "hqk,khd->qhd", weights, values_all, preferred_element_type=jnp.float32
    ).astype(jnp.bfloat16)


def ring_gather(block, axis, count, place, index):
    me = lax.axis_index(axis)
    ring, side = place(me)
    half = block.shape[0] // 2

    def send(value, step):
        perm = []
        for i in range(count):
            pos, sd = place(i)
            perm.append((i, index(pos + step, sd, i)))
        return lax.ppermute(value, axis, perm)

    def flip(value):
        perm = []
        for i in range(count):
            pos, sd = place(i)
            perm.append((i, index(pos, 1 - sd, i)))
        return lax.ppermute(value, axis, perm)

    from_minus = send(block, 1)
    from_plus = send(block, -1)
    from_y = flip(block)
    got_minus = send(jnp.concatenate([from_minus[:half], from_y]), 1)
    got_plus = send(jnp.concatenate([from_plus[half:], from_y]), -1)
    last_minus = send(got_minus[half : half + half], 1)
    last_plus = send(got_plus[half + half :], -1)
    pieces = [
        block,
        from_minus,
        from_plus,
        from_y,
        jnp.concatenate([got_minus[:half], got_plus[:half]]),
        got_minus[half:],
        got_plus[half:],
        jnp.concatenate([last_minus, last_plus]),
    ]
    sources = [
        index(ring, side, me),
        index(ring - 1, side, me),
        index(ring + 1, side, me),
        index(ring, 1 - side, me),
        index(ring + 2, side, me),
        index(ring - 1, 1 - side, me),
        index(ring + 1, 1 - side, me),
        index(ring + 2, 1 - side, me),
    ]
    return pieces, sources


def gather_rows(block, row_count):
    pieces, sources = ring_gather(
        block,
        "row",
        row_count,
        lambda r: (r // 2, r % 2),
        lambda pos, sd, r: (pos % 4) * 2 + sd,
    )
    return jnp.stack(pieces), jnp.argsort(jnp.stack(sources))


def scatter_sum(partial, col_count):
    col = lax.axis_index("col")
    chips = col_count // 2
    core = col % 2
    chip = col // 2
    blocks = partial.reshape(chips, 2, -1, partial.shape[1])
    keep = lax.dynamic_index_in_dim(blocks, core, 1, keepdims=False)
    give = lax.dynamic_index_in_dim(blocks, 1 - core, 1, keepdims=False)
    got = lax.ppermute(give.astype(jnp.bfloat16), "col", [(c, c ^ 1) for c in range(col_count)])
    half = keep + got.astype(jnp.float32)
    z_count = chips // 2
    total = lax.dynamic_index_in_dim(half, chip, 0, keepdims=False)
    for dz in range(z_count):
        for dy in range(2):
            if dz == 0 and dy == 0:
                continue
            def dest(c):
                cc = c // 2
                return (((cc // z_count) ^ dy) * z_count + (cc % z_count + dz) % z_count) * 2 + c % 2
            perm = [(c, dest(c)) for c in range(col_count)]
            target = ((chip // z_count) ^ dy) * z_count + (chip % z_count + dz) % z_count
            sent = lax.dynamic_index_in_dim(half, target, 0, keepdims=False).astype(jnp.bfloat16)
            total = total + lax.ppermute(sent, "col", perm).astype(jnp.float32)
    return total.astype(jnp.bfloat16)


def chip_offsets(chips, dy, dz):
    z_count = chips // 2

    def move(cc):
        return ((cc // z_count) ^ dy) * z_count + (cc % z_count + dz) % z_count

    return move


def gather_cols(block, col_count):
    core = lax.axis_index("col") % 2
    pieces, sources = ring_gather(
        block,
        "col",
        col_count,
        lambda c: ((c // 2) % 4, (c // 2) // 4),
        lambda pos, sd, c: (sd * 4 + pos % 4) * 2 + c % 2,
    )
    swap = [(c, c ^ 1) for c in range(col_count)]
    mates = [lax.ppermute(piece, "col", swap) for piece in pieces]
    chips = jnp.stack(sources) // 2
    holder = jnp.concatenate([chips * 2 + core, chips * 2 + 1 - core])
    return jnp.concatenate(pieces + mates, axis=1), holder


def on_device(
    inputs,
    norm_gain,
    query_train,
    key_train,
    value_train,
    out_train,
    adapter_down,
    adapter_up,
    lengths,
):
    col_count = lax.axis_size("col")
    row_count = lax.axis_size("row")
    local_rows = query_train.shape[0]
    head_local = HEADS // col_count
    merged_width = 3 * head_local * HS
    trained = jnp.stack(
        (query_train.astype(jnp.bfloat16), key_train.astype(jnp.bfloat16), value_train.astype(jnp.bfloat16)),
        axis=1,
    ).reshape(local_rows, 3, col_count, head_local * HS)
    trained = jnp.transpose(trained, (2, 0, 1, 3))
    moved = lax.all_to_all(trained, "col", 0, 0, tiled=True)
    moved = moved.reshape(col_count * local_rows, merged_width)
    moved, inputs = lax.optimization_barrier((moved, inputs))
    stacked, slot = gather_rows(moved, row_count)
    whole, holder = gather_cols(inputs, col_count)
    block_count = holder.shape[0]
    tok_count = whole.shape[0]
    gain = jnp.take(norm_gain.reshape(block_count, -1), holder, axis=0).reshape(-1)
    down = jnp.take(
        adapter_down.reshape(block_count, -1, adapter_down.shape[1]), holder, axis=0
    ).reshape(-1, adapter_down.shape[1])
    normed = normalize(whole, gain)
    adapted = jnp.dot(normed, down, preferred_element_type=jnp.float32).astype(jnp.bfloat16)
    per_row = block_count // row_count
    blocks = stacked.reshape(row_count * per_row, -1, merged_width)
    picked = jnp.take(slot, holder // per_row) * per_row + holder % per_row
    merged = jnp.take(blocks, picked, axis=0).reshape(-1, merged_width)
    out_train, merged = lax.optimization_barrier((out_train, merged))
    product = jnp.dot(normed, merged, preferred_element_type=jnp.float32)
    up_columns = adapter_up.reshape(adapter_up.shape[0], merged_width)
    joined = (product + jnp.dot(adapted, up_columns, preferred_element_type=jnp.float32)).astype(
        jnp.bfloat16
    )
    joined = joined.reshape(tok_count, 3, head_local, HS)
    segment = segment_of(lengths[0], tok_count)
    out_local = out_train.astype(jnp.bfloat16)
    out_cols = out_local.shape[1]
    out_sent = out_local.reshape(col_count, head_local * HS, out_cols)
    out_sent = jnp.broadcast_to(out_sent[None], (row_count,) + out_sent.shape).reshape(
        row_count * col_count, head_local * HS, out_cols
    )
    out_block = lax.all_to_all(out_sent, ("row", "col"), 0, 0, tiled=True)
    out_block = jnp.transpose(out_block, (1, 0, 2)).reshape(head_local * HS, -1)
    chunks = 2
    part_rows = tok_count // col_count // chunks
    position = jnp.arange(tok_count, dtype=jnp.int32)
    results = []
    for j in range(chunks):
        def pick(a):
            return a.reshape((col_count, chunks, part_rows) + a.shape[1:])[:, j].reshape(
                (-1,) + a.shape[1:]
            )

        attended = attend_rows(
            pick(joined[:, 0]), pick(position), pick(segment), joined[:, 1], joined[:, 2], segment
        )
        attended = attended.reshape(attended.shape[0], -1)
        partial_out = jnp.dot(attended, out_block, preferred_element_type=jnp.float32)
        results.append(scatter_sum(partial_out, col_count))
    return jnp.concatenate(results, axis=0)


def solution(mesh):
    in_specs = (
        P("row", "col"),
        P(),
        P(("row", "col"), None),
        P(("row", "col"), None),
        P(("row", "col"), None),
        P(None, ("row", "col")),
        P(),
        P(None, None, "col", None),
        P("row", None),
    )
    out_specs = P(("row", "col"), None)
    return jax.shard_map(
        on_device, mesh=mesh, in_specs=in_specs, out_specs=out_specs, check_vma=False
    )
```

```python
import math

import jax
import jax.numpy as jnp
from jax import lax
from jax.sharding import PartitionSpec as P

HEADS = 32
HS = 128


def normalize(whole, norm_gain):
    floats = whole.astype(jnp.float32)
    mean_square = jnp.mean(floats * floats, axis=1, keepdims=True)
    return (floats * lax.rsqrt(mean_square + 1e-05) * norm_gain).astype(jnp.bfloat16)


def segment_of(lengths_row, tok_count):
    position = jnp.arange(tok_count, dtype=jnp.int32)
    prompt_ends = jnp.cumsum(lengths_row)
    return jnp.sum((position[:, None] >= prompt_ends[None, :]).astype(jnp.int32), axis=1)


def attend(queries, keys_all, values_all, segment):
    tok_count = queries.shape[0]
    block_rows = min(512, tok_count)
    factor = 1.0 / math.sqrt(queries.shape[2])
    key_pos = jnp.arange(tok_count, dtype=jnp.int32)

    def one_block(first):
        query_blk = lax.dynamic_slice_in_dim(queries, first, block_rows, 0)
        query_pos = first + jnp.arange(block_rows, dtype=jnp.int32)
        query_seg = lax.dynamic_slice_in_dim(segment, first, block_rows, 0)
        scores = (
            jnp.einsum("qhd,khd->hqk", query_blk, keys_all, preferred_element_type=jnp.float32)
            * factor
        )
        allowed = (query_seg[:, None] == segment[None, :]) & (
            key_pos[None, :] <= query_pos[:, None]
        )
        scores = jnp.where(allowed[None], scores, -1e30)
        highest = jnp.max(scores, axis=2, keepdims=True)
        exponent = jnp.exp(scores - highest)
        weights = (exponent / jnp.sum(exponent, axis=2, keepdims=True)).astype(jnp.bfloat16)
        return jnp.einsum(
            "hqk,khd->qhd", weights, values_all, preferred_element_type=jnp.float32
        ).astype(jnp.bfloat16)

    starts = jnp.arange(tok_count // block_rows, dtype=jnp.int32) * block_rows
    blocks = lax.map(one_block, starts)
    return blocks.reshape(tok_count, queries.shape[1] * queries.shape[2])


def attend_rows(query_blk, query_pos, query_seg, keys_all, values_all, segment):
    factor = 1.0 / math.sqrt(query_blk.shape[2])
    key_pos = jnp.arange(keys_all.shape[0], dtype=jnp.int32)
    scores = (
        jnp.einsum("qhd,khd->hqk", query_blk, keys_all, preferred_element_type=jnp.float32)
        * factor
    )
    allowed = (query_seg[:, None] == segment[None, :]) & (key_pos[None, :] <= query_pos[:, None])
    scores = jnp.where(allowed[None], scores, -1e30)
    highest = jnp.max(scores, axis=2, keepdims=True)
    exponent = jnp.exp(scores - highest)
    weights = (exponent / jnp.sum(exponent, axis=2, keepdims=True)).astype(jnp.bfloat16)
    return jnp.einsum(
        "hqk,khd->qhd", weights, values_all, preferred_element_type=jnp.float32
    ).astype(jnp.bfloat16)


def ring_gather(block, axis, count, place, index):
    me = lax.axis_index(axis)
    ring, side = place(me)
    half = block.shape[0] // 2

    def send(value, step):
        perm = []
        for i in range(count):
            pos, sd = place(i)
            perm.append((i, index(pos + step, sd, i)))
        return lax.ppermute(value, axis, perm)

    def flip(value):
        perm = []
        for i in range(count):
            pos, sd = place(i)
            perm.append((i, index(pos, 1 - sd, i)))
        return lax.ppermute(value, axis, perm)

    from_minus = send(block, 1)
    from_plus = send(block, -1)
    from_y = flip(block)
    got_minus = send(jnp.concatenate([from_minus[:half], from_y]), 1)
    got_plus = send(jnp.concatenate([from_plus[half:], from_y]), -1)
    last_minus = send(got_minus[half : half + half], 1)
    last_plus = send(got_plus[half + half :], -1)
    pieces = [
        block,
        from_minus,
        from_plus,
        from_y,
        jnp.concatenate([got_minus[:half], got_plus[:half]]),
        got_minus[half:],
        got_plus[half:],
        jnp.concatenate([last_minus, last_plus]),
    ]
    sources = [
        index(ring, side, me),
        index(ring - 1, side, me),
        index(ring + 1, side, me),
        index(ring, 1 - side, me),
        index(ring + 2, side, me),
        index(ring - 1, 1 - side, me),
        index(ring + 1, 1 - side, me),
        index(ring + 2, 1 - side, me),
    ]
    return pieces, sources


def gather_rows(block, row_count):
    pieces, sources = ring_gather(
        block,
        "row",
        row_count,
        lambda r: (r // 2, r % 2),
        lambda pos, sd, r: (pos % 4) * 2 + sd,
    )
    return jnp.stack(pieces), jnp.argsort(jnp.stack(sources))


def scatter_sum(partial, col_count):
    col = lax.axis_index("col")
    chips = col_count // 2
    core = col % 2
    chip = col // 2
    blocks = partial.reshape(chips, 2, -1, partial.shape[1])
    keep = lax.dynamic_index_in_dim(blocks, core, 1, keepdims=False)
    give = lax.dynamic_index_in_dim(blocks, 1 - core, 1, keepdims=False)
    got = lax.ppermute(give.astype(jnp.bfloat16), "col", [(c, c ^ 1) for c in range(col_count)])
    half = keep + got.astype(jnp.float32)
    z_count = chips // 2
    total = lax.dynamic_index_in_dim(half, chip, 0, keepdims=False)
    for dz in range(z_count):
        for dy in range(2):
            if dz == 0 and dy == 0:
                continue
            def dest(c):
                cc = c // 2
                return (((cc // z_count) ^ dy) * z_count + (cc % z_count + dz) % z_count) * 2 + c % 2
            perm = [(c, dest(c)) for c in range(col_count)]
            target = ((chip // z_count) ^ dy) * z_count + (chip % z_count + dz) % z_count
            sent = lax.dynamic_index_in_dim(half, target, 0, keepdims=False).astype(jnp.bfloat16)
            total = total + lax.ppermute(sent, "col", perm).astype(jnp.float32)
    return total.astype(jnp.bfloat16)


def chip_offsets(chips, dy, dz):
    z_count = chips // 2

    def move(cc):
        return ((cc // z_count) ^ dy) * z_count + (cc % z_count + dz) % z_count

    return move


def gather_cols(block, col_count):
    core = lax.axis_index("col") % 2
    pieces, sources = ring_gather(
        block,
        "col",
        col_count,
        lambda c: ((c // 2) % 4, (c // 2) // 4),
        lambda pos, sd, c: (sd * 4 + pos % 4) * 2 + c % 2,
    )
    swap = [(c, c ^ 1) for c in range(col_count)]
    mates = [lax.ppermute(piece, "col", swap) for piece in pieces]
    chips = jnp.stack(sources) // 2
    holder = jnp.concatenate([chips * 2 + core, chips * 2 + 1 - core])
    return jnp.concatenate(pieces + mates, axis=1), holder


def on_device(
    inputs,
    norm_gain,
    query_train,
    key_train,
    value_train,
    out_train,
    adapter_down,
    adapter_up,
    lengths,
):
    col_count = lax.axis_size("col")
    row_count = lax.axis_size("row")
    local_rows = query_train.shape[0]
    head_local = HEADS // col_count
    merged_width = 3 * head_local * HS
    trained = jnp.stack(
        (query_train.astype(jnp.bfloat16), key_train.astype(jnp.bfloat16), value_train.astype(jnp.bfloat16)),
        axis=1,
    ).reshape(local_rows, 3, col_count, head_local * HS)
    trained = jnp.transpose(trained, (2, 0, 1, 3))
    moved = lax.all_to_all(trained, "col", 0, 0, tiled=True)
    moved = moved.reshape(col_count * local_rows, merged_width)
    stacked, slot = gather_rows(moved, row_count)
    whole, holder = gather_cols(inputs, col_count)
    block_count = holder.shape[0]
    tok_count = whole.shape[0]
    gain = jnp.take(norm_gain.reshape(block_count, -1), holder, axis=0).reshape(-1)
    down = jnp.take(
        adapter_down.reshape(block_count, -1, adapter_down.shape[1]), holder, axis=0
    ).reshape(-1, adapter_down.shape[1])
    normed = normalize(whole, gain)
    adapted = jnp.dot(normed, down, preferred_element_type=jnp.float32).astype(jnp.bfloat16)
    per_row = block_count // row_count
    blocks = stacked.reshape(row_count * per_row, -1, merged_width)
    picked = jnp.take(slot, holder // per_row) * per_row + holder % per_row
    merged = jnp.take(blocks, picked, axis=0).reshape(-1, merged_width)
    out_train, merged = lax.optimization_barrier((out_train, merged))
    product = jnp.dot(normed, merged, preferred_element_type=jnp.float32)
    up_columns = adapter_up.reshape(adapter_up.shape[0], merged_width)
    joined = (product + jnp.dot(adapted, up_columns, preferred_element_type=jnp.float32)).astype(
        jnp.bfloat16
    )
    joined = joined.reshape(tok_count, 3, head_local, HS)
    segment = segment_of(lengths[0], tok_count)
    out_local = out_train.astype(jnp.bfloat16)
    out_cols = out_local.shape[1]
    out_sent = out_local.reshape(col_count, head_local * HS, out_cols)
    out_sent = jnp.broadcast_to(out_sent[None], (row_count,) + out_sent.shape).reshape(
        row_count * col_count, head_local * HS, out_cols
    )
    out_block = lax.all_to_all(out_sent, ("row", "col"), 0, 0, tiled=True)
    out_block = jnp.transpose(out_block, (1, 0, 2)).reshape(head_local * HS, -1)
    chunks = 2
    part_rows = tok_count // col_count // chunks
    position = jnp.arange(tok_count, dtype=jnp.int32)
    results = []
    for j in range(chunks):
        def pick(a):
            return a.reshape((col_count, chunks, part_rows) + a.shape[1:])[:, j].reshape(
                (-1,) + a.shape[1:]
            )

        attended = attend_rows(
            pick(joined[:, 0]), pick(position), pick(segment), joined[:, 1], joined[:, 2], segment
        )
        attended = attended.reshape(attended.shape[0], -1)
        partial_out = jnp.dot(attended, out_block, preferred_element_type=jnp.float32)
        results.append(scatter_sum(partial_out, col_count))
    return jnp.concatenate(results, axis=0)


def solution(mesh):
    in_specs = (
        P("row", "col"),
        P(),
        P(("row", "col"), None),
        P(("row", "col"), None),
        P(("row", "col"), None),
        P(None, ("row", "col")),
        P(),
        P(None, None, "col", None),
        P("row", None),
    )
    out_specs = P(("row", "col"), None)
    return jax.shard_map(
        on_device, mesh=mesh, in_specs=in_specs, out_specs=out_specs, check_vma=False
    )
```

```python
import math

import jax
import jax.numpy as jnp
from jax import lax
from jax.sharding import PartitionSpec as P

HEADS = 32
HS = 128


def normalize(whole, norm_gain):
    floats = whole.astype(jnp.float32)
    mean_square = jnp.mean(floats * floats, axis=1, keepdims=True)
    return (floats * lax.rsqrt(mean_square + 1e-05) * norm_gain).astype(jnp.bfloat16)


def segment_of(lengths_row, tok_count):
    position = jnp.arange(tok_count, dtype=jnp.int32)
    prompt_ends = jnp.cumsum(lengths_row)
    return jnp.sum((position[:, None] >= prompt_ends[None, :]).astype(jnp.int32), axis=1)


def attend(queries, keys_all, values_all, segment):
    tok_count = queries.shape[0]
    block_rows = min(512, tok_count)
    factor = 1.0 / math.sqrt(queries.shape[2])
    key_pos = jnp.arange(tok_count, dtype=jnp.int32)

    def one_block(first):
        query_blk = lax.dynamic_slice_in_dim(queries, first, block_rows, 0)
        query_pos = first + jnp.arange(block_rows, dtype=jnp.int32)
        query_seg = lax.dynamic_slice_in_dim(segment, first, block_rows, 0)
        scores = (
            jnp.einsum("qhd,khd->hqk", query_blk, keys_all, preferred_element_type=jnp.float32)
            * factor
        )
        allowed = (query_seg[:, None] == segment[None, :]) & (
            key_pos[None, :] <= query_pos[:, None]
        )
        scores = jnp.where(allowed[None], scores, -1e30)
        highest = jnp.max(scores, axis=2, keepdims=True)
        exponent = jnp.exp(scores - highest)
        weights = (exponent / jnp.sum(exponent, axis=2, keepdims=True)).astype(jnp.bfloat16)
        return jnp.einsum(
            "hqk,khd->qhd", weights, values_all, preferred_element_type=jnp.float32
        ).astype(jnp.bfloat16)

    starts = jnp.arange(tok_count // block_rows, dtype=jnp.int32) * block_rows
    blocks = lax.map(one_block, starts)
    return blocks.reshape(tok_count, queries.shape[1] * queries.shape[2])


def attend_rows(query_blk, query_pos, query_seg, keys_all, values_all, segment):
    factor = 1.0 / math.sqrt(query_blk.shape[2])
    key_pos = jnp.arange(keys_all.shape[0], dtype=jnp.int32)
    scores = (
        jnp.einsum("qhd,khd->hqk", query_blk, keys_all, preferred_element_type=jnp.float32)
        * factor
    )
    allowed = (query_seg[:, None] == segment[None, :]) & (key_pos[None, :] <= query_pos[:, None])
    scores = jnp.where(allowed[None], scores, -1e30)
    highest = jnp.max(scores, axis=2, keepdims=True)
    exponent = jnp.exp(scores - highest)
    weights = (exponent / jnp.sum(exponent, axis=2, keepdims=True)).astype(jnp.bfloat16)
    return jnp.einsum(
        "hqk,khd->qhd", weights, values_all, preferred_element_type=jnp.float32
    ).astype(jnp.bfloat16)


def ring_gather(block, axis, count, place, index):
    me = lax.axis_index(axis)
    ring, side = place(me)
    half = block.shape[0] // 2

    def send(value, step):
        perm = []
        for i in range(count):
            pos, sd = place(i)
            perm.append((i, index(pos + step, sd, i)))
        return lax.ppermute(value, axis, perm)

    def flip(value):
        perm = []
        for i in range(count):
            pos, sd = place(i)
            perm.append((i, index(pos, 1 - sd, i)))
        return lax.ppermute(value, axis, perm)

    from_minus = send(block, 1)
    from_plus = send(block, -1)
    from_y = flip(block)
    got_minus = send(jnp.concatenate([from_minus[:half], from_y]), 1)
    got_plus = send(jnp.concatenate([from_plus[half:], from_y]), -1)
    last_minus = send(got_minus[half : half + half], 1)
    last_plus = send(got_plus[half + half :], -1)
    pieces = [
        block,
        from_minus,
        from_plus,
        from_y,
        jnp.concatenate([got_minus[:half], got_plus[:half]]),
        got_minus[half:],
        got_plus[half:],
        jnp.concatenate([last_minus, last_plus]),
    ]
    sources = [
        index(ring, side, me),
        index(ring - 1, side, me),
        index(ring + 1, side, me),
        index(ring, 1 - side, me),
        index(ring + 2, side, me),
        index(ring - 1, 1 - side, me),
        index(ring + 1, 1 - side, me),
        index(ring + 2, 1 - side, me),
    ]
    return pieces, sources


def gather_rows(block, row_count):
    pieces, sources = ring_gather(
        block,
        "row",
        row_count,
        lambda r: (r // 2, r % 2),
        lambda pos, sd, r: (pos % 4) * 2 + sd,
    )
    return jnp.stack(pieces), jnp.argsort(jnp.stack(sources))


def scatter_sum(partial, col_count):
    col = lax.axis_index("col")
    chips = col_count // 2
    core = col % 2
    chip = col // 2
    blocks = partial.reshape(chips, 2, -1, partial.shape[1])
    keep = lax.dynamic_index_in_dim(blocks, core, 1, keepdims=False)
    give = lax.dynamic_index_in_dim(blocks, 1 - core, 1, keepdims=False)
    got = lax.ppermute(give.astype(jnp.bfloat16), "col", [(c, c ^ 1) for c in range(col_count)])
    half = keep + got.astype(jnp.float32)
    return half


def scatter_cross(half, col_count):
    col = lax.axis_index("col")
    chips = col_count // 2
    chip = col // 2
    z_count = chips // 2
    total = lax.dynamic_index_in_dim(half, chip, 0, keepdims=False)
    for dz in range(z_count):
        for dy in range(2):
            if dz == 0 and dy == 0:
                continue
            def dest(c):
                cc = c // 2
                return (((cc // z_count) ^ dy) * z_count + (cc % z_count + dz) % z_count) * 2 + c % 2
            perm = [(c, dest(c)) for c in range(col_count)]
            target = ((chip // z_count) ^ dy) * z_count + (chip % z_count + dz) % z_count
            sent = lax.dynamic_index_in_dim(half, target, 0, keepdims=False).astype(jnp.bfloat16)
            total = total + lax.ppermute(sent, "col", perm).astype(jnp.float32)
    return total.astype(jnp.bfloat16)


def chip_offsets(chips, dy, dz):
    z_count = chips // 2

    def move(cc):
        return ((cc // z_count) ^ dy) * z_count + (cc % z_count + dz) % z_count

    return move


def gather_cols(block, col_count):
    core = lax.axis_index("col") % 2
    pieces, sources = ring_gather(
        block,
        "col",
        col_count,
        lambda c: ((c // 2) % 4, (c // 2) // 4),
        lambda pos, sd, c: (sd * 4 + pos % 4) * 2 + c % 2,
    )
    swap = [(c, c ^ 1) for c in range(col_count)]
    mates = [lax.ppermute(piece, "col", swap) for piece in pieces]
    chips = jnp.stack(sources) // 2
    holder = jnp.concatenate([chips * 2 + core, chips * 2 + 1 - core])
    return jnp.concatenate(pieces + mates, axis=1), holder


def on_device(
    inputs,
    norm_gain,
    query_train,
    key_train,
    value_train,
    out_train,
    adapter_down,
    adapter_up,
    lengths,
):
    col_count = lax.axis_size("col")
    row_count = lax.axis_size("row")
    local_rows = query_train.shape[0]
    head_local = HEADS // col_count
    merged_width = 3 * head_local * HS
    trained = jnp.stack(
        (query_train.astype(jnp.bfloat16), key_train.astype(jnp.bfloat16), value_train.astype(jnp.bfloat16)),
        axis=1,
    ).reshape(local_rows, 3, col_count, head_local * HS)
    trained = jnp.transpose(trained, (2, 0, 1, 3))
    moved = lax.all_to_all(trained, "col", 0, 0, tiled=True)
    moved = moved.reshape(col_count * local_rows, merged_width)
    moved, inputs = lax.optimization_barrier((moved, inputs))
    stacked, slot = gather_rows(moved, row_count)
    whole, holder = gather_cols(inputs, col_count)
    block_count = holder.shape[0]
    tok_count = whole.shape[0]
    gain = jnp.take(norm_gain.reshape(block_count, -1), holder, axis=0).reshape(-1)
    down = jnp.take(
        adapter_down.reshape(block_count, -1, adapter_down.shape[1]), holder, axis=0
    ).reshape(-1, adapter_down.shape[1])
    normed = normalize(whole, gain)
    adapted = jnp.dot(normed, down, preferred_element_type=jnp.float32).astype(jnp.bfloat16)
    per_row = block_count // row_count
    blocks = stacked.reshape(row_count * per_row, -1, merged_width)
    picked = jnp.take(slot, holder // per_row) * per_row + holder % per_row
    merged = jnp.take(blocks, picked, axis=0).reshape(-1, merged_width)
    out_train, merged = lax.optimization_barrier((out_train, merged))
    product = jnp.dot(normed, merged, preferred_element_type=jnp.float32)
    up_columns = adapter_up.reshape(adapter_up.shape[0], merged_width)
    joined = (product + jnp.dot(adapted, up_columns, preferred_element_type=jnp.float32)).astype(
        jnp.bfloat16
    )
    joined = joined.reshape(tok_count, 3, head_local, HS)
    segment = segment_of(lengths[0], tok_count)
    out_local = out_train.astype(jnp.bfloat16)
    out_cols = out_local.shape[1]
    out_sent = out_local.reshape(col_count, head_local * HS, out_cols)
    out_sent = jnp.broadcast_to(out_sent[None], (row_count,) + out_sent.shape).reshape(
        row_count * col_count, head_local * HS, out_cols
    )
    out_block = lax.all_to_all(out_sent, ("row", "col"), 0, 0, tiled=True)
    out_block = jnp.transpose(out_block, (1, 0, 2)).reshape(head_local * HS, -1)
    chunks = 2
    part_rows = tok_count // col_count // chunks
    position = jnp.arange(tok_count, dtype=jnp.int32)
    results = []
    for j in range(chunks):
        def pick(a):
            return a.reshape((col_count, chunks, part_rows) + a.shape[1:])[:, j].reshape(
                (-1,) + a.shape[1:]
            )

        attended = attend_rows(
            pick(joined[:, 0]), pick(position), pick(segment), joined[:, 1], joined[:, 2], segment
        )
        attended = attended.reshape(attended.shape[0], -1)
        partial_out = jnp.dot(attended, out_block, preferred_element_type=jnp.float32)
        results.append(scatter_sum(partial_out, col_count))
    return scatter_cross(jnp.concatenate(results, axis=1), col_count)


def solution(mesh):
    in_specs = (
        P("row", "col"),
        P(),
        P(("row", "col"), None),
        P(("row", "col"), None),
        P(("row", "col"), None),
        P(None, ("row", "col")),
        P(),
        P(None, None, "col", None),
        P("row", None),
    )
    out_specs = P(("row", "col"), None)
    return jax.shard_map(
        on_device, mesh=mesh, in_specs=in_specs, out_specs=out_specs, check_vma=False
    )
```

```python
import math

import jax
import jax.numpy as jnp
from jax import lax
from jax.sharding import PartitionSpec as P

HEADS = 32
HS = 128


def normalize(whole, norm_gain):
    floats = whole.astype(jnp.float32)
    mean_square = jnp.mean(floats * floats, axis=1, keepdims=True)
    return (floats * lax.rsqrt(mean_square + 1e-05) * norm_gain).astype(jnp.bfloat16)


def segment_of(lengths_row, tok_count):
    position = jnp.arange(tok_count, dtype=jnp.int32)
    prompt_ends = jnp.cumsum(lengths_row)
    return jnp.sum((position[:, None] >= prompt_ends[None, :]).astype(jnp.int32), axis=1)


def attend(queries, keys_all, values_all, segment):
    tok_count = queries.shape[0]
    block_rows = min(512, tok_count)
    factor = 1.0 / math.sqrt(queries.shape[2])
    key_pos = jnp.arange(tok_count, dtype=jnp.int32)

    def one_block(first):
        query_blk = lax.dynamic_slice_in_dim(queries, first, block_rows, 0)
        query_pos = first + jnp.arange(block_rows, dtype=jnp.int32)
        query_seg = lax.dynamic_slice_in_dim(segment, first, block_rows, 0)
        scores = (
            jnp.einsum("qhd,khd->hqk", query_blk, keys_all, preferred_element_type=jnp.float32)
            * factor
        )
        allowed = (query_seg[:, None] == segment[None, :]) & (
            key_pos[None, :] <= query_pos[:, None]
        )
        scores = jnp.where(allowed[None], scores, -1e30)
        highest = jnp.max(scores, axis=2, keepdims=True)
        exponent = jnp.exp(scores - highest)
        weights = (exponent / jnp.sum(exponent, axis=2, keepdims=True)).astype(jnp.bfloat16)
        return jnp.einsum(
            "hqk,khd->qhd", weights, values_all, preferred_element_type=jnp.float32
        ).astype(jnp.bfloat16)

    starts = jnp.arange(tok_count // block_rows, dtype=jnp.int32) * block_rows
    blocks = lax.map(one_block, starts)
    return blocks.reshape(tok_count, queries.shape[1] * queries.shape[2])


def attend_rows(query_blk, query_pos, query_seg, keys_all, values_all, segment):
    factor = 1.0 / math.sqrt(query_blk.shape[2])
    key_pos = jnp.arange(keys_all.shape[0], dtype=jnp.int32)
    scores = (
        jnp.einsum("qhd,khd->hqk", query_blk, keys_all, preferred_element_type=jnp.float32)
        * factor
    )
    allowed = (query_seg[:, None] == segment[None, :]) & (key_pos[None, :] <= query_pos[:, None])
    scores = jnp.where(allowed[None], scores, -1e30)
    highest = jnp.max(scores, axis=2, keepdims=True)
    exponent = jnp.exp(scores - highest)
    weights = (exponent / jnp.sum(exponent, axis=2, keepdims=True)).astype(jnp.bfloat16)
    return jnp.einsum(
        "hqk,khd->qhd", weights, values_all, preferred_element_type=jnp.float32
    ).astype(jnp.bfloat16)


def ring_gather(block, axis, count, place, index):
    me = lax.axis_index(axis)
    ring, side = place(me)
    half = block.shape[0] // 2

    def send(value, step):
        perm = []
        for i in range(count):
            pos, sd = place(i)
            perm.append((i, index(pos + step, sd, i)))
        return lax.ppermute(value, axis, perm)

    def flip(value):
        perm = []
        for i in range(count):
            pos, sd = place(i)
            perm.append((i, index(pos, 1 - sd, i)))
        return lax.ppermute(value, axis, perm)

    from_minus = send(block, 1)
    from_plus = send(block, -1)
    from_y = flip(block)
    got_minus = send(jnp.concatenate([from_minus[:half], from_y]), 1)
    got_plus = send(jnp.concatenate([from_plus[half:], from_y]), -1)
    last_minus = send(got_minus[half : half + half], 1)
    last_plus = send(got_plus[half + half :], -1)
    pieces = [
        block,
        from_minus,
        from_plus,
        from_y,
        jnp.concatenate([got_minus[:half], got_plus[:half]]),
        got_minus[half:],
        got_plus[half:],
        jnp.concatenate([last_minus, last_plus]),
    ]
    sources = [
        index(ring, side, me),
        index(ring - 1, side, me),
        index(ring + 1, side, me),
        index(ring, 1 - side, me),
        index(ring + 2, side, me),
        index(ring - 1, 1 - side, me),
        index(ring + 1, 1 - side, me),
        index(ring + 2, 1 - side, me),
    ]
    return pieces, sources


def gather_rows(block, row_count):
    pieces, sources = ring_gather(
        block,
        "row",
        row_count,
        lambda r: (r // 2, r % 2),
        lambda pos, sd, r: (pos % 4) * 2 + sd,
    )
    return jnp.stack(pieces), jnp.argsort(jnp.stack(sources))


def scatter_sum(partial, col_count):
    col = lax.axis_index("col")
    chips = col_count // 2
    core = col % 2
    chip = col // 2
    blocks = partial.reshape(chips, 2, -1, partial.shape[1])
    keep = lax.dynamic_index_in_dim(blocks, core, 1, keepdims=False)
    give = lax.dynamic_index_in_dim(blocks, 1 - core, 1, keepdims=False)
    got = lax.ppermute(give.astype(jnp.bfloat16), "col", [(c, c ^ 1) for c in range(col_count)])
    half = keep + got.astype(jnp.float32)
    z_count = chips // 2
    total = lax.dynamic_index_in_dim(half, chip, 0, keepdims=False)
    for dz in range(z_count):
        for dy in range(2):
            if dz == 0 and dy == 0:
                continue
            def dest(c):
                cc = c // 2
                return (((cc // z_count) ^ dy) * z_count + (cc % z_count + dz) % z_count) * 2 + c % 2
            perm = [(c, dest(c)) for c in range(col_count)]
            target = ((chip // z_count) ^ dy) * z_count + (chip % z_count + dz) % z_count
            sent = lax.dynamic_index_in_dim(half, target, 0, keepdims=False).astype(jnp.bfloat16)
            total = total + lax.ppermute(sent, "col", perm).astype(jnp.float32)
    return total.astype(jnp.bfloat16)


def chip_offsets(chips, dy, dz):
    z_count = chips // 2

    def move(cc):
        return ((cc // z_count) ^ dy) * z_count + (cc % z_count + dz) % z_count

    return move


def gather_cols(block, col_count):
    core = lax.axis_index("col") % 2
    pieces, sources = ring_gather(
        block,
        "col",
        col_count,
        lambda c: ((c // 2) % 4, (c // 2) // 4),
        lambda pos, sd, c: (sd * 4 + pos % 4) * 2 + c % 2,
    )
    swap = [(c, c ^ 1) for c in range(col_count)]
    mates = [lax.ppermute(piece, "col", swap) for piece in pieces]
    chips = jnp.stack(sources) // 2
    holder = jnp.concatenate([chips * 2 + core, chips * 2 + 1 - core])
    return jnp.concatenate(pieces + mates, axis=1), holder, pieces[1]


def on_device(
    inputs,
    norm_gain,
    query_train,
    key_train,
    value_train,
    out_train,
    adapter_down,
    adapter_up,
    lengths,
):
    col_count = lax.axis_size("col")
    row_count = lax.axis_size("row")
    local_rows = query_train.shape[0]
    head_local = HEADS // col_count
    merged_width = 3 * head_local * HS
    trained = jnp.stack(
        (query_train.astype(jnp.bfloat16), key_train.astype(jnp.bfloat16), value_train.astype(jnp.bfloat16)),
        axis=1,
    ).reshape(local_rows, 3, col_count, head_local * HS)
    trained = jnp.transpose(trained, (2, 0, 1, 3))
    moved = lax.all_to_all(trained, "col", 0, 0, tiled=True)
    moved = moved.reshape(col_count * local_rows, merged_width)
    moved, inputs = lax.optimization_barrier((moved, inputs))
    stacked, slot = gather_rows(moved, row_count)
    whole, holder, first = gather_cols(inputs, col_count)
    out_train, first = lax.optimization_barrier((out_train, first))
    block_count = holder.shape[0]
    tok_count = whole.shape[0]
    gain = jnp.take(norm_gain.reshape(block_count, -1), holder, axis=0).reshape(-1)
    down = jnp.take(
        adapter_down.reshape(block_count, -1, adapter_down.shape[1]), holder, axis=0
    ).reshape(-1, adapter_down.shape[1])
    normed = normalize(whole, gain)
    adapted = jnp.dot(normed, down, preferred_element_type=jnp.float32).astype(jnp.bfloat16)
    per_row = block_count // row_count
    blocks = stacked.reshape(row_count * per_row, -1, merged_width)
    picked = jnp.take(slot, holder // per_row) * per_row + holder % per_row
    merged = jnp.take(blocks, picked, axis=0).reshape(-1, merged_width)
    product = jnp.dot(normed, merged, preferred_element_type=jnp.float32)
    up_columns = adapter_up.reshape(adapter_up.shape[0], merged_width)
    joined = (product + jnp.dot(adapted, up_columns, preferred_element_type=jnp.float32)).astype(
        jnp.bfloat16
    )
    joined = joined.reshape(tok_count, 3, head_local, HS)
    segment = segment_of(lengths[0], tok_count)
    out_local = out_train.astype(jnp.bfloat16)
    out_cols = out_local.shape[1]
    out_sent = out_local.reshape(col_count, head_local * HS, out_cols)
    out_sent = jnp.broadcast_to(out_sent[None], (row_count,) + out_sent.shape).reshape(
        row_count * col_count, head_local * HS, out_cols
    )
    out_block = lax.all_to_all(out_sent, ("row", "col"), 0, 0, tiled=True)
    out_block = jnp.transpose(out_block, (1, 0, 2)).reshape(head_local * HS, -1)
    chunks = 2
    part_rows = tok_count // col_count // chunks
    position = jnp.arange(tok_count, dtype=jnp.int32)
    results = []
    for j in range(chunks):
        def pick(a):
            return a.reshape((col_count, chunks, part_rows) + a.shape[1:])[:, j].reshape(
                (-1,) + a.shape[1:]
            )

        attended = attend_rows(
            pick(joined[:, 0]), pick(position), pick(segment), joined[:, 1], joined[:, 2], segment
        )
        attended = attended.reshape(attended.shape[0], -1)
        partial_out = jnp.dot(attended, out_block, preferred_element_type=jnp.float32)
        results.append(scatter_sum(partial_out, col_count))
    return jnp.concatenate(results, axis=0)


def solution(mesh):
    in_specs = (
        P("row", "col"),
        P(),
        P(("row", "col"), None),
        P(("row", "col"), None),
        P(("row", "col"), None),
        P(None, ("row", "col")),
        P(),
        P(None, None, "col", None),
        P("row", None),
    )
    out_specs = P(("row", "col"), None)
    return jax.shard_map(
        on_device, mesh=mesh, in_specs=in_specs, out_specs=out_specs, check_vma=False
    )
```
